128 devices in a mesh: row: 16 (over z_lo, x, core), col: 8 (over y, z_hi).
Axes of the slice: x: 4, y: 4, z: 4 (z_hi: 2, z_lo: 2; z = z_hi * 2 + z_lo), core: 2. Of those that a mesh axis runs over, the one named last changes fastest.
Arguments:
- slab_embed: float32 [65536, 768], P(('col', 'row')), may hold values from -1 to 1
- coverage_old: float32 [65536], P('col'), may hold values from 2 to 4.5
- sel_index: int32 [2048], P('row'), may hold values from 0 to 65535
- cand_index: int32 [3072], P('row'), may hold values from 0 to 65535
Outputs:
- coverage: float32 [65536], P('col')
- total_gain: float32 [3072], P('row')
The draws below stay inside these ranges and needn't reach their ends.
Inputs may be any that keep to these rules, and one draw needn't show every extreme that they name: `sel_index`: indices into the slab. `cand_index`: indices into the slab.
All inputs are finite; a program needn't handle non-finite values.
Results may differ from the reference program's by a relative error of at most 0.00014.
Values sent between devices are 32-bit elements; how exact they have to be, the bound alone decides.
No kernel may reach another device: no remote copies, remote signals or barrier semaphores. Data moves between devices by JAX's collectives and lax.ppermute only.
A program may use at most 128 MiB of HBM per device.

```python
import jax
import jax.numpy as jnp
from jax import lax

D = 768
N = 65536
K = 3072
S = 2048
N_COL = 8


def plant(array, key, low, largest):
    longest = array.shape.index(max(array.shape))
    spots = []
    for shift in (0, 1):
        where = [jax.random.randint(jax.random.fold_in(key, axis), (), 0, length) for axis, length in enumerate(array.shape)]
        where[longest] = (where[longest] + shift) % array.shape[longest]
        spots.append(tuple(where))
    return array.at[spots[0]].set(low).at[spots[1]].set(largest)


def levels(stream_key, dims, cuts, low, top_value):
    level, own = 1.0, jax.random.fold_in(stream_key, 6)
    for axis_at, parts in cuts:
        steps = jnp.exp(jax.random.uniform(jax.random.fold_in(own, axis_at), (parts,), jnp.float32, low / len(cuts), top_value / len(cuts)))
        level = level * jnp.repeat(steps, dims[axis_at] // parts).reshape([-1 if axis == axis_at else 1 for axis in range(len(dims))])
    return level


def noise(key, dims, deviation, limit, split=(), held_as=jnp.bfloat16):
    entries = deviation * jax.random.normal(key, dims, jnp.float32)
    if split:
        entries = entries * levels(key, dims, split, -0.22, 0.18)
    return jnp.clip(entries, -limit, limit).astype(held_as)


def setup_inputs(seed: int = 0) -> dict:
    splits = jax.random.split(jax.random.key(seed), 5)
    slab_embed = noise(splits[0], (N, D), 0.19, 1.0, ((0, 128),), jnp.float32)
    coverage_old = jnp.clip(2.0 + 2.5 * jax.random.uniform(splits[1], (N,), jnp.float32) ** levels(splits[1], (N,), ((0, 8),), -0.2, 0.2), 2.0, 4.5)
    sel_index = plant(jax.random.randint(splits[2], (S,), 0, N), jax.random.fold_in(splits[2], 1), 0, N - 1).astype(jnp.int32)
    cand_index = plant(jax.random.randint(splits[3], (K,), 0, N), jax.random.fold_in(splits[3], 1), 0, N - 1).astype(jnp.int32)
    return {"slab_embed": slab_embed, "coverage_old": coverage_old, "sel_index": sel_index, "cand_index": cand_index}


def similar(left, right):
    return lax.dot_general(left, right, (((1,), (1,)), ((), ())), precision=lax.Precision.HIGHEST, preferred_element_type=jnp.float32)


def reference(slab_embed, coverage_old, sel_index, cand_index):
    selected = jnp.take(slab_embed, sel_index, axis=0)
    chosen = jnp.take(slab_embed, cand_index, axis=0)
    blocks = slab_embed.reshape(N_COL, -1, D)
    old_blocks = coverage_old.reshape(N_COL, -1)

    def per_block(packed):
        points, previous = packed
        reached = jnp.max(similar(selected, points), axis=0)
        updated = jnp.maximum(previous, reached)
        scores = similar(chosen, points)
        return updated, jnp.sum(jnp.maximum(scores - updated[None, :], 0.0), axis=1)

    covered, partial_value = lax.map(per_block, (blocks, old_blocks))
    return covered.reshape(-1), jnp.sum(partial_value, axis=0)
```

```python
import jax
import jax.numpy as jnp
from jax import lax
from jax.sharding import PartitionSpec as P


def similar(left, right):
    return lax.dot_general(
        left,
        right,
        (((1,), (1,)), ((), ())),
        precision=lax.Precision.HIGH,
        preferred_element_type=jnp.float32,
    )


def lookup(source, indices, first_row):
    position = indices - first_row
    inside = (position >= 0) & (position < source.shape[0])
    picked = jnp.take(source, jnp.clip(position, 0, source.shape[0] - 1), axis=0)
    return jnp.where(inside[:, None], picked, 0.0)


def shift(value, axis, size, pairs):
    return lax.ppermute(value, axis, [(i, j) for i, j in pairs if i < size and j < size])


def col_parts(value, n_y, n_z):
    size = n_y * n_z
    here = lax.axis_index("col")
    y, z = here // n_z, here % n_z
    if n_z == 2:
        other = shift(value, "col", size, [(c, c ^ 1) for c in range(size)])
        pair = jnp.where(z == 0, jnp.stack([value, other]), jnp.stack([other, value]))
    else:
        pair = value[None]
    if n_y == 1:
        return pair
    up = [(c, ((c // n_z + 1) % n_y) * n_z + c % n_z) for c in range(size)]
    down = [(c, ((c // n_z - 1) % n_y) * n_z + c % n_z) for c in range(size)]
    from_below = shift(pair, "col", size, up)
    from_above = shift(pair, "col", size, down)
    parts = [pair, from_above, None, from_below]
    if n_y == 4:
        parts[2] = shift(from_below, "col", size, up)
        ordered = jnp.stack(parts)
    else:
        ordered = jnp.stack([pair, from_above])
    return jnp.roll(ordered, y, axis=0).reshape((size,) + value.shape)


def col_masked_sum(value, n_y, n_z):
    size = n_y * n_z
    if n_z == 2:
        value = value + shift(value, "col", size, [(c, c ^ 1) for c in range(size)])
    up = [(c, ((c // n_z + 1) % n_y) * n_z + c % n_z) for c in range(size)]
    down = [(c, ((c // n_z - 1) % n_y) * n_z + c % n_z) for c in range(size)]
    from_below = shift(value, "col", size, up)
    from_above = shift(value, "col", size, down)
    far = shift(from_below, "col", size, up)
    return value + from_below + from_above + far


def row_max(value, n):
    here = lax.axis_index("row")
    value = jnp.maximum(value, shift(value, "row", n, [(r, r ^ 1) for r in range(n)]))
    x_up = [(r, (r & ~6) | ((((r >> 1) & 3) + 1) % 4) << 1) for r in range(n)]
    x_down = [(r, (r & ~6) | ((((r >> 1) & 3) - 1) % 4) << 1) for r in range(n)]
    value = jnp.maximum(value, jnp.maximum(shift(value, "row", n, x_up), shift(value, "row", n, x_down)))
    value = jnp.maximum(value, shift(value, "row", n, x_up))
    value = jnp.maximum(value, shift(value, "row", n, [(r, r ^ 8) for r in range(n)]))
    return value


def body(slab_embed, coverage_old, sel_index, cand_index):
    col_id = lax.axis_index("col")
    gathered = lax.all_gather(slab_embed, "row", axis=0, tiled=True)
    first_row = col_id * gathered.shape[0]
    n_sel = sel_index.shape[0]
    picked = col_masked_sum(
        jnp.concatenate([lookup(gathered, sel_index, first_row), lookup(gathered, cand_index, first_row)]), 4, 2
    )
    selected, chosen = picked[:n_sel], picked[n_sel:]
    partial_value = jnp.max(similar(selected, gathered), axis=0)
    reached = row_max(partial_value, 16)
    coverage = jnp.maximum(coverage_old, reached)
    gain_part = jnp.sum(jnp.maximum(similar(chosen, gathered) - coverage[None, :], 0.0), axis=1)
    total_gain = jnp.sum(col_parts(gain_part, 4, 2), axis=0)
    return (coverage, total_gain)


def solution(mesh):
    in_specs = (P(("col", "row"), None), P("col"), P("row"), P("row"))
    out_specs = (P("col"), P("row"))
    return jax.shard_map(body, mesh=mesh, in_specs=in_specs, out_specs=out_specs, check_vma=False)
```

```python
import jax
import jax.numpy as jnp
from jax import lax
from jax.sharding import PartitionSpec as P

N_Y, N_Z = 4, 2


def similar(left, right):
    return lax.dot_general(
        left,
        right,
        (((1,), (1,)), ((), ())),
        precision=lax.Precision.HIGH,
        preferred_element_type=jnp.float32,
    )


def lookup(source, indices, first_row):
    position = indices - first_row
    inside = (position >= 0) & (position < source.shape[0])
    picked = jnp.take(source, jnp.clip(position, 0, source.shape[0] - 1), axis=0)
    return jnp.where(inside[:, None], picked, 0.0)


def col_of(y, z):
    return (y % N_Y) * N_Z + z


def y_shift(value, step):
    pairs = [(col_of(y, z), col_of(y + step, z)) for y in range(N_Y) for z in range(N_Z)]
    return lax.ppermute(value, "col", pairs)


def col_masked_sum(value):
    here = lax.axis_index("col")
    y, z = here // N_Z, here % N_Z
    half = value.shape[0] // N_Z
    quarter = half // N_Y
    halves = value.reshape(N_Z, half, *value.shape[1:])
    mine = jnp.where(z == 0, halves[0], halves[1])
    theirs = jnp.where(z == 0, halves[1], halves[0])
    mine = mine + lax.ppermute(theirs, "col", [(c, c ^ 1) for c in range(N_Y * N_Z)])

    def part(k):
        return lax.dynamic_slice_in_dim(mine, ((y + k) % N_Y) * quarter, quarter)

    own = part(0)
    for k in range(1, N_Y):
        own = own + y_shift(part(k), k)
    pieces = [own] + [y_shift(own, -k) for k in range(1, N_Y)]
    ordered = jnp.roll(jnp.stack(pieces), y, axis=0).reshape(half, *value.shape[1:])
    other = lax.ppermute(ordered, "col", [(c, c ^ 1) for c in range(N_Y * N_Z)])
    return jnp.where(z == 0, jnp.concatenate([ordered, other]), jnp.concatenate([other, ordered]))


def all_max(value, axis, n):
    result = value
    for k in range(1, n):
        result = jnp.maximum(result, lax.ppermute(value, axis, [(i, i ^ k) for i in range(n)]))
    return result


def all_sum(value, axis, n):
    here = lax.axis_index(axis)
    parts = jnp.stack([value] + [lax.ppermute(value, axis, [(i, i ^ k) for i in range(n)]) for k in range(1, n)])
    ordered = jnp.take(parts, jnp.arange(n) ^ here, axis=0)
    return jnp.sum(ordered, axis=0)


def body(slab_embed, coverage_old, sel_index, cand_index):
    n_row = 16
    col_id = lax.axis_index("col")
    gathered = lax.all_gather(slab_embed, "row", axis=0, tiled=True)
    first_row = col_id * gathered.shape[0]
    selected = col_masked_sum(lookup(gathered, sel_index, first_row))
    chosen = col_masked_sum(lookup(gathered, cand_index, first_row))
    partial_value = jnp.max(similar(selected, gathered), axis=0)
    reached = all_max(partial_value, "row", n_row)
    coverage = jnp.maximum(coverage_old, reached)
    gain_part = jnp.sum(jnp.maximum(similar(chosen, gathered) - coverage[None, :], 0.0), axis=1)
    total_gain = all_sum(gain_part, "col", N_Y * N_Z)
    return (coverage, total_gain)


def solution(mesh):
    in_specs = (P(("col", "row"), None), P("col"), P("row"), P("row"))
    out_specs = (P("col"), P("row"))
    return jax.shard_map(body, mesh=mesh, in_specs=in_specs, out_specs=out_specs, check_vma=False)
```

```python
import jax
import jax.numpy as jnp
from jax import lax
from jax.sharding import PartitionSpec as P

N_Y, N_Z = 4, 2


def similar(left, right):
    return lax.dot_general(
        left,
        right,
        (((1,), (1,)), ((), ())),
        precision=lax.Precision.HIGH,
        preferred_element_type=jnp.float32,
    )


def lookup(source, indices, first_row):
    position = indices - first_row
    inside = (position >= 0) & (position < source.shape[0])
    picked = jnp.take(source, jnp.clip(position, 0, source.shape[0] - 1), axis=0)
    return jnp.where(inside[:, None], picked, 0.0)


def col_of(y, z):
    return (y % N_Y) * N_Z + z


def y_shift(value, step):
    pairs = [(col_of(y, z), col_of(y + step, z)) for y in range(N_Y) for z in range(N_Z)]
    return lax.ppermute(value, "col", pairs)


def col_masked_sum(value):
    here = lax.axis_index("col")
    y, z = here // N_Z, here % N_Z
    half = value.shape[0] // N_Z
    quarter = half // N_Y
    halves = value.reshape(N_Z, half, *value.shape[1:])
    mine = jnp.where(z == 0, halves[0], halves[1])
    theirs = jnp.where(z == 0, halves[1], halves[0])
    mine = mine + lax.ppermute(theirs, "col", [(c, c ^ 1) for c in range(N_Y * N_Z)])

    def part(k):
        return lax.dynamic_slice_in_dim(mine, ((y + k) % N_Y) * quarter, quarter)

    own = part(0)
    for k in range(1, N_Y):
        own = own + y_shift(part(k), k)
    pieces = [own] + [y_shift(own, -k) for k in range(1, N_Y)]
    ordered = jnp.roll(jnp.stack(pieces), y, axis=0).reshape(half, *value.shape[1:])
    other = lax.ppermute(ordered, "col", [(c, c ^ 1) for c in range(N_Y * N_Z)])
    return jnp.where(z == 0, jnp.concatenate([ordered, other]), jnp.concatenate([other, ordered]))


def all_max(value, axis, n):
    bit = 1
    while bit < n:
        value = jnp.maximum(value, lax.ppermute(value, axis, [(i, i ^ bit) for i in range(n)]))
        bit *= 2
    return value


def all_sum(value, axis, n):
    here = lax.axis_index(axis)
    parts = value[None]
    bit = 1
    while bit < n:
        other = lax.ppermute(parts, axis, [(i, i ^ bit) for i in range(n)])
        low = (here & bit) == 0
        parts = jnp.where(low, jnp.concatenate([parts, other]), jnp.concatenate([other, parts]))
        bit *= 2
    return jnp.sum(parts, axis=0)


def body(slab_embed, coverage_old, sel_index, cand_index):
    n_row = 16
    col_id = lax.axis_index("col")
    gathered = lax.all_gather(slab_embed, "row", axis=0, tiled=True)
    first_row = col_id * gathered.shape[0]
    selected = col_masked_sum(lookup(gathered, sel_index, first_row))
    chosen = col_masked_sum(lookup(gathered, cand_index, first_row))
    n_chunks = 2
    width = gathered.shape[0] // n_chunks
    coverages, gains = [], []
    for i in range(n_chunks):
        points = gathered[i * width:(i + 1) * width]
        reached = all_max(jnp.max(similar(selected, points), axis=0), "row", n_row)
        coverage = jnp.maximum(coverage_old[i * width:(i + 1) * width], reached)
        coverages.append(coverage)
        gains.append(jnp.sum(jnp.maximum(similar(chosen, points) - coverage[None, :], 0.0), axis=1))
    total_gain = all_sum(sum(gains[1:], gains[0]), "col", N_Y * N_Z)
    return (jnp.concatenate(coverages), total_gain)


def solution(mesh):
    in_specs = (P(("col", "row"), None), P("col"), P("row"), P("row"))
    out_specs = (P("col"), P("row"))
    return jax.shard_map(body, mesh=mesh, in_specs=in_specs, out_specs=out_specs, check_vma=False)
```

```python
import jax
import jax.numpy as jnp
from jax import lax
from jax.sharding import PartitionSpec as P

N_Y, N_Z = 4, 2


def similar(left, right):
    return lax.dot_general(
        left,
        right,
        (((1,), (1,)), ((), ())),
        precision=lax.Precision.HIGH,
        preferred_element_type=jnp.float32,
    )


def lookup(source, indices, first_row):
    position = indices - first_row
    inside = (position >= 0) & (position < source.shape[0])
    picked = jnp.take(source, jnp.clip(position, 0, source.shape[0] - 1), axis=0)
    return jnp.where(inside[:, None], picked, 0.0)


def col_of(y, z):
    return (y % N_Y) * N_Z + z


def y_shift(value, step):
    pairs = [(col_of(y, z), col_of(y + step, z)) for y in range(N_Y) for z in range(N_Z)]
    return lax.ppermute(value, "col", pairs)


def col_masked_sum(value):
    here = lax.axis_index("col")
    y, z = here // N_Z, here % N_Z
    half = value.shape[0] // N_Z
    quarter = half // N_Y
    halves = value.reshape(N_Z, half, *value.shape[1:])
    mine = jnp.where(z == 0, halves[0], halves[1])
    theirs = jnp.where(z == 0, halves[1], halves[0])
    mine = mine + lax.ppermute(theirs, "col", [(c, c ^ 1) for c in range(N_Y * N_Z)])

    def part(k):
        return lax.dynamic_slice_in_dim(mine, ((y + k) % N_Y) * quarter, quarter)

    own = part(0)
    for k in range(1, N_Y):
        own = own + y_shift(part(k), k)
    pieces = [own] + [y_shift(own, -k) for k in range(1, N_Y)]
    ordered = jnp.roll(jnp.stack(pieces), y, axis=0).reshape(half, *value.shape[1:])
    other = lax.ppermute(ordered, "col", [(c, c ^ 1) for c in range(N_Y * N_Z)])
    return jnp.where(z == 0, jnp.concatenate([ordered, other]), jnp.concatenate([other, ordered]))


def all_max(value, axis, n):
    bit = 1
    while bit < n:
        value = jnp.maximum(value, lax.ppermute(value, axis, [(i, i ^ bit) for i in range(n)]))
        bit *= 2
    return value


def all_sum(value, axis, n):
    here = lax.axis_index(axis)
    parts = value[None]
    bit = 1
    while bit < n:
        other = lax.ppermute(parts, axis, [(i, i ^ bit) for i in range(n)])
        low = (here & bit) == 0
        parts = jnp.where(low, jnp.concatenate([parts, other]), jnp.concatenate([other, parts]))
        bit *= 2
    return jnp.sum(parts, axis=0)


def body(slab_embed, coverage_old, sel_index, cand_index):
    n_row = 16
    col_id = lax.axis_index("col")
    gathered = lax.all_gather(slab_embed, "row", axis=0, tiled=True)
    first_row = col_id * gathered.shape[0]
    n_sel = sel_index.shape[0]
    picked = col_masked_sum(
        jnp.concatenate([lookup(gathered, sel_index, first_row), lookup(gathered, cand_index, first_row)])
    )
    selected, chosen = picked[:n_sel], picked[n_sel:]
    n_chunks = 1
    width = gathered.shape[0] // n_chunks
    coverages, gains = [], []
    for i in range(n_chunks):
        points = gathered[i * width:(i + 1) * width]
        reached = all_max(jnp.max(similar(selected, points), axis=0), "row", n_row)
        coverage = jnp.maximum(coverage_old[i * width:(i + 1) * width], reached)
        coverages.append(coverage)
        gains.append(jnp.sum(jnp.maximum(similar(chosen, points) - coverage[None, :], 0.0), axis=1))
    total_gain = all_sum(sum(gains[1:], gains[0]), "col", N_Y * N_Z)
    return (jnp.concatenate(coverages), total_gain)


def solution(mesh):
    in_specs = (P(("col", "row"), None), P("col"), P("row"), P("row"))
    out_specs = (P("col"), P("row"))
    return jax.shard_map(body, mesh=mesh, in_specs=in_specs, out_specs=out_specs, check_vma=False)
```

```python
import jax
import jax.numpy as jnp
from jax import lax
from jax.experimental import pallas as pl
from jax.experimental.pallas import tpu as pltpu
from jax.sharding import PartitionSpec as P

N_Y, N_Z = 4, 2


def similar(left, right):
    return lax.dot_general(
        left,
        right,
        (((1,), (1,)), ((), ())),
        precision=lax.Precision.HIGH,
        preferred_element_type=jnp.float32,
    )


def row_copy_kernel(position_ref, source_ref, out_ref, sem):
    count = out_ref.shape[0]

    def issue(i, carry):
        pltpu.make_async_copy(source_ref.at[pl.ds(position_ref[i], 1)], out_ref.at[pl.ds(i, 1)], sem).start()
        return carry

    lax.fori_loop(0, count, issue, 0)
    pltpu.make_async_copy(source_ref.at[pl.ds(0, count)], out_ref, sem).wait()


def take_rows(source, positions):
    return pl.pallas_call(
        row_copy_kernel,
        grid_spec=pltpu.PrefetchScalarGridSpec(
            num_scalar_prefetch=1,
            grid=(1,),
            in_specs=[pl.BlockSpec(memory_space=pl.ANY)],
            out_specs=pl.BlockSpec(memory_space=pl.ANY),
            scratch_shapes=[pltpu.SemaphoreType.DMA(())],
        ),
        out_shape=jax.ShapeDtypeStruct((positions.shape[0], source.shape[1]), source.dtype),
    )(positions, source)


def lookup(source, indices, first_row):
    position = indices - first_row
    inside = (position >= 0) & (position < source.shape[0])
    picked = take_rows(source, jnp.clip(position, 0, source.shape[0] - 1))
    return jnp.where(inside[:, None], picked, 0.0)


def col_of(y, z):
    return (y % N_Y) * N_Z + z


def y_shift(value, step):
    pairs = [(col_of(y, z), col_of(y + step, z)) for y in range(N_Y) for z in range(N_Z)]
    return lax.ppermute(value, "col", pairs)


def col_masked_sum(value):
    here = lax.axis_index("col")
    y, z = here // N_Z, here % N_Z
    half = value.shape[0] // N_Z
    quarter = half // N_Y
    halves = value.reshape(N_Z, half, *value.shape[1:])
    mine = jnp.where(z == 0, halves[0], halves[1])
    theirs = jnp.where(z == 0, halves[1], halves[0])
    mine = mine + lax.ppermute(theirs, "col", [(c, c ^ 1) for c in range(N_Y * N_Z)])

    def part(k):
        return lax.dynamic_slice_in_dim(mine, ((y + k) % N_Y) * quarter, quarter)

    own = part(0)
    for k in range(1, N_Y):
        own = own + y_shift(part(k), k)
    pieces = [own] + [y_shift(own, -k) for k in range(1, N_Y)]
    ordered = jnp.roll(jnp.stack(pieces), y, axis=0).reshape(half, *value.shape[1:])
    other = lax.ppermute(ordered, "col", [(c, c ^ 1) for c in range(N_Y * N_Z)])
    return jnp.where(z == 0, jnp.concatenate([ordered, other]), jnp.concatenate([other, ordered]))


def all_max(value, axis, n):
    bit = 1
    while bit < n:
        value = jnp.maximum(value, lax.ppermute(value, axis, [(i, i ^ bit) for i in range(n)]))
        bit *= 2
    return value


def all_sum(value, axis, n):
    here = lax.axis_index(axis)
    parts = value[None]
    bit = 1
    while bit < n:
        other = lax.ppermute(parts, axis, [(i, i ^ bit) for i in range(n)])
        low = (here & bit) == 0
        parts = jnp.where(low, jnp.concatenate([parts, other]), jnp.concatenate([other, parts]))
        bit *= 2
    return jnp.sum(parts, axis=0)


def body(slab_embed, coverage_old, sel_index, cand_index):
    n_row = 16
    col_id = lax.axis_index("col")
    gathered = lax.all_gather(slab_embed, "row", axis=0, tiled=True)
    first_row = col_id * gathered.shape[0]
    n_sel = sel_index.shape[0]
    picked = col_masked_sum(lookup(gathered, jnp.concatenate([sel_index, cand_index]), first_row))
    selected, chosen = picked[:n_sel], picked[n_sel:]
    n_chunks = 1
    width = gathered.shape[0] // n_chunks
    coverages, gains = [], []
    for i in range(n_chunks):
        points = gathered[i * width:(i + 1) * width]
        reached = all_max(jnp.max(similar(selected, points), axis=0), "row", n_row)
        coverage = jnp.maximum(coverage_old[i * width:(i + 1) * width], reached)
        coverages.append(coverage)
        gains.append(jnp.sum(jnp.maximum(similar(chosen, points) - coverage[None, :], 0.0), axis=1))
    total_gain = all_sum(sum(gains[1:], gains[0]), "col", N_Y * N_Z)
    return (jnp.concatenate(coverages), total_gain)


def solution(mesh):
    in_specs = (P(("col", "row"), None), P("col"), P("row"), P("row"))
    out_specs = (P("col"), P("row"))
    return jax.shard_map(body, mesh=mesh, in_specs=in_specs, out_specs=out_specs, check_vma=False)
```

```python
import jax
import jax.numpy as jnp
from jax import lax
from jax.sharding import PartitionSpec as P

N_Y, N_Z = 4, 2


def similar(left, right):
    return lax.dot_general(
        left,
        right,
        (((1,), (1,)), ((), ())),
        precision=lax.Precision.HIGH,
        preferred_element_type=jnp.float32,
    )


def lookup(source, indices, first_row):
    position = indices - first_row
    inside = (position >= 0) & (position < source.shape[0])
    picked = jnp.take(source, jnp.clip(position, 0, source.shape[0] - 1), axis=0)
    return jnp.where(inside[:, None], picked, 0.0)


def col_of(y, z):
    return (y % N_Y) * N_Z + z


def y_shift(value, step):
    pairs = [(col_of(y, z), col_of(y + step, z)) for y in range(N_Y) for z in range(N_Z)]
    return lax.ppermute(value, "col", pairs)


def col_masked_sum(value):
    here = lax.axis_index("col")
    y, z = here // N_Z, here % N_Z
    quarter = value.shape[0] // N_Y
    half = quarter // N_Z

    def part(k):
        return lax.dynamic_slice_in_dim(value, ((y + k) % N_Y) * quarter, quarter)

    own = part(0)
    for k in range(1, N_Y):
        own = own + y_shift(part(k), k)
    halves = own.reshape(N_Z, half, *value.shape[1:])
    mine = jnp.where(z == 0, halves[0], halves[1])
    theirs = jnp.where(z == 0, halves[1], halves[0])
    swap = [(c, c ^ 1) for c in range(N_Y * N_Z)]
    mine = mine + lax.ppermute(theirs, "col", swap)
    other = lax.ppermute(mine, "col", swap)
    own = jnp.where(z == 0, jnp.concatenate([mine, other]), jnp.concatenate([other, mine]))
    pieces = [own] + [y_shift(own, -k) for k in range(1, N_Y)]
    return jnp.roll(jnp.stack(pieces), y, axis=0).reshape(value.shape)


def all_max(value, axis, n):
    bit = 1
    while bit < n:
        value = jnp.maximum(value, lax.ppermute(value, axis, [(i, i ^ bit) for i in range(n)]))
        bit *= 2
    return value


def all_sum(value, axis, n):
    here = lax.axis_index(axis)
    parts = value[None]
    bit = 1
    while bit < n:
        other = lax.ppermute(parts, axis, [(i, i ^ bit) for i in range(n)])
        low = (here & bit) == 0
        parts = jnp.where(low, jnp.concatenate([parts, other]), jnp.concatenate([other, parts]))
        bit *= 2
    return jnp.sum(parts, axis=0)


def body(slab_embed, coverage_old, sel_index, cand_index):
    n_row = 16
    col_id = lax.axis_index("col")
    gathered = lax.all_gather(slab_embed, "row", axis=0, tiled=True)
    first_row = col_id * gathered.shape[0]
    n_sel = sel_index.shape[0]
    picked = col_masked_sum(
        jnp.concatenate([lookup(gathered, sel_index, first_row), lookup(gathered, cand_index, first_row)])
    )
    selected, chosen = picked[:n_sel], picked[n_sel:]
    n_chunks = 1
    width = gathered.shape[0] // n_chunks
    coverages, gains = [], []
    for i in range(n_chunks):
        points = gathered[i * width:(i + 1) * width]
        reached = all_max(jnp.max(similar(selected, points), axis=0), "row", n_row)
        coverage = jnp.maximum(coverage_old[i * width:(i + 1) * width], reached)
        coverages.append(coverage)
        gains.append(jnp.sum(jnp.maximum(similar(chosen, points) - coverage[None, :], 0.0), axis=1))
    total_gain = all_sum(sum(gains[1:], gains[0]), "col", N_Y * N_Z)
    return (jnp.concatenate(coverages), total_gain)


def solution(mesh):
    in_specs = (P(("col", "row"), None), P("col"), P("row"), P("row"))
    out_specs = (P("col"), P("row"))
    return jax.shard_map(body, mesh=mesh, in_specs=in_specs, out_specs=out_specs, check_vma=False)
```

```python
import jax
import jax.numpy as jnp
from jax import lax
from jax.sharding import PartitionSpec as P

N_Y, N_Z = 4, 2


def similar(left, right):
    return lax.dot_general(
        left,
        right,
        (((1,), (1,)), ((), ())),
        precision=lax.Precision.HIGH,
        preferred_element_type=jnp.float32,
    )


def lookup(source, indices, first_row):
    position = indices - first_row
    inside = (position >= 0) & (position < source.shape[0])
    picked = jnp.take(source, jnp.clip(position, 0, source.shape[0] - 1), axis=0)
    return jnp.where(inside[:, None], picked, 0.0)


def col_of(y, z):
    return (y % N_Y) * N_Z + z


def y_shift(value, step):
    pairs = [(col_of(y, z), col_of(y + step, z)) for y in range(N_Y) for z in range(N_Z)]
    return lax.ppermute(value, "col", pairs)


def col_masked_sum(value):
    here = lax.axis_index("col")
    y, z = here // N_Z, here % N_Z
    quarter = value.shape[0] // N_Y
    half = quarter // N_Z

    def part(k):
        return lax.dynamic_slice_in_dim(value, ((y + k) % N_Y) * quarter, quarter)

    own = part(0)
    for k in range(1, N_Y):
        own = own + y_shift(part(k), k)
    halves = own.reshape(N_Z, half, *value.shape[1:])
    mine = jnp.where(z == 0, halves[0], halves[1])
    theirs = jnp.where(z == 0, halves[1], halves[0])
    swap = [(c, c ^ 1) for c in range(N_Y * N_Z)]
    mine = mine + lax.ppermute(theirs, "col", swap)
    other = lax.ppermute(mine, "col", swap)
    own = jnp.where(z == 0, jnp.concatenate([mine, other]), jnp.concatenate([other, mine]))
    pieces = [own] + [y_shift(own, -k) for k in range(1, N_Y)]
    return jnp.roll(jnp.stack(pieces), y, axis=0).reshape(value.shape)


def all_max(value, axis, n):
    bit = 1
    while bit < n:
        value = jnp.maximum(value, lax.ppermute(value, axis, [(i, i ^ bit) for i in range(n)]))
        bit *= 2
    return value


def all_sum(value, axis, n):
    here = lax.axis_index(axis)
    parts = value[None]
    bit = 1
    while bit < n:
        other = lax.ppermute(parts, axis, [(i, i ^ bit) for i in range(n)])
        low = (here & bit) == 0
        parts = jnp.where(low, jnp.concatenate([parts, other]), jnp.concatenate([other, parts]))
        bit *= 2
    return jnp.sum(parts, axis=0)


def body(slab_embed, coverage_old, sel_index, cand_index):
    n_row = 16
    col_id = lax.axis_index("col")
    gathered = lax.all_gather(slab_embed, "row", axis=0, tiled=True)
    first_row = col_id * gathered.shape[0]
    selected = col_masked_sum(lookup(gathered, sel_index, first_row))
    chosen = col_masked_sum(lookup(gathered, cand_index, first_row))
    reached = all_max(jnp.max(similar(selected, gathered), axis=0), "row", n_row)
    coverages = [jnp.maximum(coverage_old, reached)]
    scores = lax.optimization_barrier(similar(chosen, gathered))
    gain_part = jnp.sum(jnp.maximum(scores - coverages[0][None, :], 0.0), axis=1)
    total_gain = all_sum(gain_part, "col", N_Y * N_Z)
    return (jnp.concatenate(coverages), total_gain)


def solution(mesh):
    in_specs = (P(("col", "row"), None), P("col"), P("row"), P("row"))
    out_specs = (P("col"), P("row"))
    return jax.shard_map(body, mesh=mesh, in_specs=in_specs, out_specs=out_specs, check_vma=False)
```

```python
import jax
import jax.numpy as jnp
from jax import lax
from jax.sharding import Mesh
from jax.sharding import PartitionSpec as P

N_Y, N_Z = 4, 2


def similar(left, right):
    return lax.dot_general(
        left,
        right,
        (((1,), (1,)), ((), ())),
        precision=lax.Precision.HIGH,
        preferred_element_type=jnp.float32,
    )


def lookup(source, indices, first_row):
    position = indices - first_row
    inside = (position >= 0) & (position < source.shape[0])
    picked = jnp.take(source, jnp.clip(position, 0, source.shape[0] - 1), axis=0)
    return jnp.where(inside[:, None], picked, 0.0)


def col_of(y, z):
    return (y % N_Y) * N_Z + z


def y_shift(value, step):
    pairs = [(col_of(y, z), col_of(y + step, z)) for y in range(N_Y) for z in range(N_Z)]
    return lax.ppermute(value, "col", pairs)


def pair_split(value, low):
    halves = value.reshape(2, value.shape[0] // 2, *value.shape[1:])
    return jnp.where(low, halves[0], halves[1]), jnp.where(low, halves[1], halves[0])


def pair_join(mine, other, low):
    return jnp.where(low, jnp.concatenate([mine, other]), jnp.concatenate([other, mine]))


def group_masked_sum(value):
    here = lax.axis_index("col")
    y, z = here // N_Z, here % N_Z
    zl = lax.axis_index("zl")
    quarter = value.shape[0] // N_Y

    def part(k):
        return lax.dynamic_slice_in_dim(value, ((y + k) % N_Y) * quarter, quarter)

    own = part(0)
    for k in range(1, N_Y):
        own = own + y_shift(part(k), k)
    zl_swap = [(0, 1), (1, 0)]
    z_swap = [(c, c ^ 1) for c in range(N_Y * N_Z)]
    mine, theirs = pair_split(own, zl == 0)
    mine = mine + lax.ppermute(theirs, "zl", zl_swap)
    low, high = pair_split(mine, z == 0)
    low = low + lax.ppermute(high, "col", z_swap)
    mine = pair_join(low, lax.ppermute(low, "col", z_swap), z == 0)
    own = pair_join(mine, lax.ppermute(mine, "zl", zl_swap), zl == 0)
    pieces = [own] + [y_shift(own, -k) for k in range(1, N_Y)]
    return jnp.roll(jnp.stack(pieces), y, axis=0).reshape(value.shape)


def all_max(value, axis, n):
    bit = 1
    while bit < n:
        value = jnp.maximum(value, lax.ppermute(value, axis, [(i, i ^ bit) for i in range(n)]))
        bit *= 2
    return value


def gather_in_order(parts, axis, n):
    here = lax.axis_index(axis)
    bit = 1
    while bit < n:
        other = lax.ppermute(parts, axis, [(i, i ^ bit) for i in range(n)])
        low = (here & bit) == 0
        parts = jnp.where(low, jnp.concatenate([parts, other]), jnp.concatenate([other, parts]))
        bit *= 2
    return parts


def body(slab_embed, coverage_old, sel_index, cand_index):
    n_xc = 8
    col_id = lax.axis_index("col")
    zl = lax.axis_index("zl")
    half = lax.all_gather(slab_embed, "xc", axis=0, tiled=True)
    first_row = (col_id * 2 + zl) * half.shape[0]
    zl_swap = [(0, 1), (1, 0)]
    both_sel = pair_join(sel_index, lax.ppermute(sel_index, "zl", zl_swap), zl == 0)
    both_cand = pair_join(cand_index, lax.ppermute(cand_index, "zl", zl_swap), zl == 0)
    selected = group_masked_sum(lookup(half, both_sel, first_row))
    chosen = group_masked_sum(lookup(half, both_cand, first_row))
    reached = all_max(jnp.max(similar(selected, half), axis=0), "xc", n_xc)
    old = lax.dynamic_slice_in_dim(coverage_old, zl * half.shape[0], half.shape[0])
    coverage = jnp.maximum(old, reached)
    scores = lax.optimization_barrier(similar(chosen, half))
    gain_part = jnp.sum(jnp.maximum(scores - coverage[None, :], 0.0), axis=1)
    parts = gather_in_order(gather_in_order(gain_part[None], "zl", 2)[None], "col", N_Y * N_Z)
    total = jnp.sum(parts.reshape(-1, gain_part.shape[0]), axis=0)
    total_gain = lax.dynamic_slice_in_dim(total, zl * cand_index.shape[0], cand_index.shape[0])
    full_coverage = pair_join(coverage, lax.ppermute(coverage, "zl", zl_swap), zl == 0)
    return (full_coverage, total_gain)


def solution(mesh):
    shape = dict(zip(mesh.axis_names, mesh.devices.shape))
    names, sizes = [], []
    for name in mesh.axis_names:
        if name == "row":
            names += ["zl", "xc"]
            sizes += [2, shape["row"] // 2]
        else:
            names.append(name)
            sizes.append(shape[name])
    split = Mesh(mesh.devices.reshape(sizes), tuple(names))
    in_specs = (P(("col", "zl", "xc"), None), P("col"), P(("zl", "xc")), P(("zl", "xc")))
    out_specs = (P("col"), P(("zl", "xc")))
    return jax.shard_map(body, mesh=split, in_specs=in_specs, out_specs=out_specs, check_vma=False)
```

```python
import jax
import jax.numpy as jnp
from jax import lax
from jax.sharding import Mesh
from jax.sharding import PartitionSpec as P

N_Y, N_Z = 4, 2


def similar(left, right):
    return lax.dot_general(
        left,
        right,
        (((1,), (1,)), ((), ())),
        precision=lax.Precision.HIGH,
        preferred_element_type=jnp.float32,
    )


def lookup(source, indices, first_row):
    position = indices - first_row
    inside = (position >= 0) & (position < source.shape[0])
    picked = jnp.take(source, jnp.clip(position, 0, source.shape[0] - 1), axis=0)
    return jnp.where(inside[:, None], picked, 0.0)


def col_of(y, z):
    return (y % N_Y) * N_Z + z


def y_shift(value, step):
    pairs = [(col_of(y, z), col_of(y + step, z)) for y in range(N_Y) for z in range(N_Z)]
    return lax.ppermute(value, "col", pairs)


def pair_split(value, low):
    halves = value.reshape(2, value.shape[0] // 2, *value.shape[1:])
    return jnp.where(low, halves[0], halves[1]), jnp.where(low, halves[1], halves[0])


def pair_join(mine, other, low):
    return jnp.where(low, jnp.concatenate([mine, other]), jnp.concatenate([other, mine]))


def group_masked_sum(value):
    here = lax.axis_index("col")
    y, z = here // N_Z, here % N_Z
    zl = lax.axis_index("zl")
    quarter = value.shape[0] // N_Y

    def part(k):
        return lax.dynamic_slice_in_dim(value, ((y + k) % N_Y) * quarter, quarter)

    own = part(0)
    for k in range(1, N_Y):
        own = own + y_shift(part(k), k)
    zl_swap = [(0, 1), (1, 0)]
    z_swap = [(c, c ^ 1) for c in range(N_Y * N_Z)]
    mine, theirs = pair_split(own, zl == 0)
    mine = mine + lax.ppermute(theirs, "zl", zl_swap)
    low, high = pair_split(mine, z == 0)
    low = low + lax.ppermute(high, "col", z_swap)
    mine = pair_join(low, lax.ppermute(low, "col", z_swap), z == 0)
    own = pair_join(mine, lax.ppermute(mine, "zl", zl_swap), zl == 0)
    pieces = [own] + [y_shift(own, -k) for k in range(1, N_Y)]
    return jnp.roll(jnp.stack(pieces), y, axis=0).reshape(value.shape)


def all_max(value, axis, n):
    bit = 1
    while bit < n:
        value = jnp.maximum(value, lax.ppermute(value, axis, [(i, i ^ bit) for i in range(n)]))
        bit *= 2
    return value


def gather_in_order(parts, axis, n):
    here = lax.axis_index(axis)
    bit = 1
    while bit < n:
        other = lax.ppermute(parts, axis, [(i, i ^ bit) for i in range(n)])
        low = (here & bit) == 0
        parts = jnp.where(low, jnp.concatenate([parts, other]), jnp.concatenate([other, parts]))
        bit *= 2
    return parts


def body(slab_embed, coverage_old, sel_index, cand_index):
    n_xc = 8
    col_id = lax.axis_index("col")
    zl = lax.axis_index("zl")
    half = lax.all_gather(slab_embed, "xc", axis=0, tiled=True)
    first_row = (col_id * 2 + zl) * half.shape[0]
    zl_swap = [(0, 1), (1, 0)]
    both_sel = pair_join(sel_index, lax.ppermute(sel_index, "zl", zl_swap), zl == 0)
    both_cand = pair_join(cand_index, lax.ppermute(cand_index, "zl", zl_swap), zl == 0)
    n_sel = both_sel.shape[0]
    picked = group_masked_sum(lookup(half, jnp.concatenate([both_sel, both_cand]), first_row))
    scores = lax.optimization_barrier(similar(picked, half))
    reached = all_max(jnp.max(scores[:n_sel], axis=0), "xc", n_xc)
    old = lax.dynamic_slice_in_dim(coverage_old, zl * half.shape[0], half.shape[0])
    coverage = jnp.maximum(old, reached)
    gain_part = jnp.sum(jnp.maximum(scores[n_sel:] - coverage[None, :], 0.0), axis=1)
    parts = gather_in_order(gather_in_order(gain_part[None], "zl", 2)[None], "col", N_Y * N_Z)
    total = jnp.sum(parts.reshape(-1, gain_part.shape[0]), axis=0)
    total_gain = lax.dynamic_slice_in_dim(total, zl * cand_index.shape[0], cand_index.shape[0])
    full_coverage = pair_join(coverage, lax.ppermute(coverage, "zl", zl_swap), zl == 0)
    return (full_coverage, total_gain)


def solution(mesh):
    shape = dict(zip(mesh.axis_names, mesh.devices.shape))
    names, sizes = [], []
    for name in mesh.axis_names:
        if name == "row":
            names += ["zl", "xc"]
            sizes += [2, shape["row"] // 2]
        else:
            names.append(name)
            sizes.append(shape[name])
    split = Mesh(mesh.devices.reshape(sizes), tuple(names))
    in_specs = (P(("col", "zl", "xc"), None), P("col"), P(("zl", "xc")), P(("zl", "xc")))
    out_specs = (P("col"), P(("zl", "xc")))
    return jax.shard_map(body, mesh=split, in_specs=in_specs, out_specs=out_specs, check_vma=False)
```

```python
import jax
import jax.numpy as jnp
from jax import lax
from jax.sharding import Mesh
from jax.sharding import PartitionSpec as P

N_Y, N_Z = 4, 2


def similar(left, right):
    return lax.dot_general(
        left,
        right,
        (((1,), (1,)), ((), ())),
        precision=lax.Precision.HIGH,
        preferred_element_type=jnp.float32,
    )


def lookup(source, indices, first_row):
    position = indices - first_row
    inside = (position >= 0) & (position < source.shape[0])
    picked = jnp.take(source, jnp.clip(position, 0, source.shape[0] - 1), axis=0)
    return jnp.where(inside[:, None], picked, 0.0)


def col_of(y, z):
    return (y % N_Y) * N_Z + z


def y_shift(value, step):
    pairs = [(col_of(y, z), col_of(y + step, z)) for y in range(N_Y) for z in range(N_Z)]
    return lax.ppermute(value, "col", pairs)


def pair_split(value, low):
    halves = value.reshape(2, value.shape[0] // 2, *value.shape[1:])
    return jnp.where(low, halves[0], halves[1]), jnp.where(low, halves[1], halves[0])


def pair_join(mine, other, low):
    return jnp.where(low, jnp.concatenate([mine, other]), jnp.concatenate([other, mine]))


def group_masked_sum(value):
    here = lax.axis_index("col")
    y, z = here // N_Z, here % N_Z
    zl = lax.axis_index("zl")
    quarter = value.shape[0] // N_Y

    def part(k):
        return lax.dynamic_slice_in_dim(value, ((y + k) % N_Y) * quarter, quarter)

    own = part(0)
    for k in range(1, N_Y):
        own = own + y_shift(part(k), k)
    zl_swap = [(0, 1), (1, 0)]
    z_swap = [(c, c ^ 1) for c in range(N_Y * N_Z)]
    mine, theirs = pair_split(own, zl == 0)
    mine = mine + lax.ppermute(theirs, "zl", zl_swap)
    low, high = pair_split(mine, z == 0)
    low = low + lax.ppermute(high, "col", z_swap)
    mine = pair_join(low, lax.ppermute(low, "col", z_swap), z == 0)
    own = pair_join(mine, lax.ppermute(mine, "zl", zl_swap), zl == 0)
    pieces = [own] + [y_shift(own, -k) for k in range(1, N_Y)]
    return jnp.roll(jnp.stack(pieces), y, axis=0).reshape(value.shape)


def all_max(value, axis, n):
    bit = 1
    while bit < n:
        value = jnp.maximum(value, lax.ppermute(value, axis, [(i, i ^ bit) for i in range(n)]))
        bit *= 2
    return value


def gather_in_order(parts, axis, n):
    here = lax.axis_index(axis)
    bit = 1
    while bit < n:
        other = lax.ppermute(parts, axis, [(i, i ^ bit) for i in range(n)])
        low = (here & bit) == 0
        parts = jnp.where(low, jnp.concatenate([parts, other]), jnp.concatenate([other, parts]))
        bit *= 2
    return parts


def body(slab_embed, coverage_old, sel_index, cand_index):
    n_xc = 8
    col_id = lax.axis_index("col")
    zl = lax.axis_index("zl")
    half = lax.all_gather(slab_embed, "xc", axis=0, tiled=True)
    first_row = (col_id * 2 + zl) * half.shape[0]
    zl_swap = [(0, 1), (1, 0)]
    both_sel = pair_join(sel_index, lax.ppermute(sel_index, "zl", zl_swap), zl == 0)
    both_cand = pair_join(cand_index, lax.ppermute(cand_index, "zl", zl_swap), zl == 0)
    selected = group_masked_sum(lookup(half, both_sel, first_row))
    chosen = group_masked_sum(lookup(half, both_cand, first_row))
    n_sel = both_sel.shape[0]
    scores = lax.optimization_barrier(similar(jnp.concatenate([selected, chosen]), half))
    reached = all_max(jnp.max(scores[:n_sel], axis=0), "xc", n_xc)
    old = lax.dynamic_slice_in_dim(coverage_old, zl * half.shape[0], half.shape[0])
    coverage = jnp.maximum(old, reached)
    gain_part = jnp.sum(jnp.maximum(scores[n_sel:] - coverage[None, :], 0.0), axis=1)
    parts = gather_in_order(gather_in_order(gain_part[None], "zl", 2)[None], "col", N_Y * N_Z)
    total = jnp.sum(parts.reshape(-1, gain_part.shape[0]), axis=0)
    total_gain = lax.dynamic_slice_in_dim(total, zl * cand_index.shape[0], cand_index.shape[0])
    full_coverage = pair_join(coverage, lax.ppermute(coverage, "zl", zl_swap), zl == 0)
    return (full_coverage, total_gain)


def solution(mesh):
    shape = dict(zip(mesh.axis_names, mesh.devices.shape))
    names, sizes = [], []
    for name in mesh.axis_names:
        if name == "row":
            names += ["zl", "xc"]
            sizes += [2, shape["row"] // 2]
        else:
            names.append(name)
            sizes.append(shape[name])
    split = Mesh(mesh.devices.reshape(sizes), tuple(names))
    in_specs = (P(("col", "zl", "xc"), None), P("col"), P(("zl", "xc")), P(("zl", "xc")))
    out_specs = (P("col"), P(("zl", "xc")))
    return jax.shard_map(body, mesh=split, in_specs=in_specs, out_specs=out_specs, check_vma=False)
```

```python
import jax
import jax.numpy as jnp
from jax import lax
from jax.sharding import Mesh
from jax.sharding import PartitionSpec as P

N_Y, N_Z = 4, 2


def similar(left, right):
    return lax.dot_general(
        left,
        right,
        (((1,), (1,)), ((), ())),
        precision=lax.Precision.HIGH,
        preferred_element_type=jnp.float32,
    )


def lookup(source, indices, first_row):
    position = indices - first_row
    inside = (position >= 0) & (position < source.shape[0])
    picked = jnp.take(source, jnp.clip(position, 0, source.shape[0] - 1), axis=0)
    return jnp.where(inside[:, None], picked, 0.0)


def col_of(y, z):
    return (y % N_Y) * N_Z + z


def y_shift(value, step):
    pairs = [(col_of(y, z), col_of(y + step, z)) for y in range(N_Y) for z in range(N_Z)]
    return lax.ppermute(value, "col", pairs)


def pair_split(value, low):
    halves = value.reshape(2, value.shape[0] // 2, *value.shape[1:])
    return jnp.where(low, halves[0], halves[1]), jnp.where(low, halves[1], halves[0])


def pair_join(mine, other, low):
    return jnp.where(low, jnp.concatenate([mine, other]), jnp.concatenate([other, mine]))


def group_masked_sum(value):
    here = lax.axis_index("col")
    y, z = here // N_Z, here % N_Z
    zl = lax.axis_index("zl")
    quarter = value.shape[0] // N_Y

    def part(k):
        return lax.dynamic_slice_in_dim(value, ((y + k) % N_Y) * quarter, quarter)

    own = part(0)
    for k in range(1, N_Y):
        own = own + y_shift(part(k), k)
    zl_swap = [(0, 1), (1, 0)]
    z_swap = [(c, c ^ 1) for c in range(N_Y * N_Z)]
    mine, theirs = pair_split(own, zl == 0)
    mine = mine + lax.ppermute(theirs, "zl", zl_swap)
    low, high = pair_split(mine, z == 0)
    low = low + lax.ppermute(high, "col", z_swap)
    mine = pair_join(low, lax.ppermute(low, "col", z_swap), z == 0)
    own = pair_join(mine, lax.ppermute(mine, "zl", zl_swap), zl == 0)
    pieces = [own] + [y_shift(own, -k) for k in range(1, N_Y)]
    return jnp.roll(jnp.stack(pieces), y, axis=0).reshape(value.shape)


def all_max(value, axis, n):
    bit = 1
    while bit < n:
        value = jnp.maximum(value, lax.ppermute(value, axis, [(i, i ^ bit) for i in range(n)]))
        bit *= 2
    return value


def gather_in_order(parts, axis, n):
    here = lax.axis_index(axis)
    bit = 1
    while bit < n:
        other = lax.ppermute(parts, axis, [(i, i ^ bit) for i in range(n)])
        low = (here & bit) == 0
        parts = jnp.where(low, jnp.concatenate([parts, other]), jnp.concatenate([other, parts]))
        bit *= 2
    return parts


def x_shift(value, step, n_x):
    pairs = [(i, ((i // 2 + step) % n_x) * 2 + i % 2) for i in range(2 * n_x)]
    return lax.ppermute(value, "xc", pairs)


def xc_gather(shard, n_x):
    here = lax.axis_index("xc")
    core = here % 2
    die = [(i, i ^ 1) for i in range(2 * n_x)]
    rows = shard.shape[0] // 2
    from_below = x_shift(shard, 1, n_x)
    from_above = x_shift(shard, -1, n_x)
    other = lax.ppermute(shard, "xc", die)
    far = jnp.concatenate([x_shift(from_below[:rows], 1, n_x), x_shift(from_above[rows:], -1, n_x)])
    near = lax.ppermute(jnp.stack([from_above, from_below]), "xc", die)
    other_far = lax.ppermute(far, "xc", die)
    mine = jnp.stack([shard, from_above, far, from_below])
    theirs = jnp.stack([other, near[0], other_far, near[1]])
    both = jnp.where(core == 0, jnp.stack([mine, theirs], axis=1), jnp.stack([theirs, mine], axis=1))
    return both.reshape(-1, shard.shape[1])


def body(slab_embed, coverage_old, sel_index, cand_index):
    n_xc = 8
    col_id = lax.axis_index("col")
    zl = lax.axis_index("zl")
    n_x = n_xc // 2
    x = lax.axis_index("xc") // 2
    shard_rows = slab_embed.shape[0]
    half = xc_gather(slab_embed, n_x)
    first_row = (col_id * 2 + zl) * half.shape[0]

    def to_local(index):
        canonical = index - first_row
        source = (jnp.clip(canonical, 0, half.shape[0] - 1) // shard_rows) // 2
        offset = (source - x) % n_x
        return jnp.where(
            (canonical >= 0) & (canonical < half.shape[0]),
            offset * 2 * shard_rows + canonical % (2 * shard_rows),
            -1,
        )

    zl_swap = [(0, 1), (1, 0)]
    both_sel = pair_join(sel_index, lax.ppermute(sel_index, "zl", zl_swap), zl == 0)
    both_cand = pair_join(cand_index, lax.ppermute(cand_index, "zl", zl_swap), zl == 0)
    selected = group_masked_sum(lookup(half, to_local(both_sel), 0))
    chosen = group_masked_sum(lookup(half, to_local(both_cand), 0))
    n_sel = both_sel.shape[0]
    scores = lax.optimization_barrier(similar(jnp.concatenate([selected, chosen]), half))
    partial = jnp.roll(jnp.max(scores[:n_sel], axis=0).reshape(n_x, -1), x, axis=0).reshape(-1)
    reached = all_max(partial, "xc", n_xc)
    old = lax.dynamic_slice_in_dim(coverage_old, zl * half.shape[0], half.shape[0])
    coverage = jnp.maximum(old, reached)
    local_coverage = jnp.roll(coverage.reshape(n_x, -1), -x, axis=0).reshape(-1)
    gain_part = jnp.sum(jnp.maximum(scores[n_sel:] - local_coverage[None, :], 0.0), axis=1)
    parts = gather_in_order(gather_in_order(gain_part[None], "zl", 2)[None], "col", N_Y * N_Z)
    total = jnp.sum(parts.reshape(-1, gain_part.shape[0]), axis=0)
    total_gain = lax.dynamic_slice_in_dim(total, zl * cand_index.shape[0], cand_index.shape[0])
    full_coverage = pair_join(coverage, lax.ppermute(coverage, "zl", zl_swap), zl == 0)
    return (full_coverage, total_gain)


def solution(mesh):
    shape = dict(zip(mesh.axis_names, mesh.devices.shape))
    names, sizes = [], []
    for name in mesh.axis_names:
        if name == "row":
            names += ["zl", "xc"]
            sizes += [2, shape["row"] // 2]
        else:
            names.append(name)
            sizes.append(shape[name])
    split = Mesh(mesh.devices.reshape(sizes), tuple(names))
    in_specs = (P(("col", "zl", "xc"), None), P("col"), P(("zl", "xc")), P(("zl", "xc")))
    out_specs = (P("col"), P(("zl", "xc")))
    return jax.shard_map(body, mesh=split, in_specs=in_specs, out_specs=out_specs, check_vma=False)
```

```python
import jax
import jax.numpy as jnp
from jax import lax
from jax.sharding import Mesh
from jax.sharding import PartitionSpec as P

N_Y, N_Z = 4, 2


def similar(left, right):
    return lax.dot_general(
        left,
        right,
        (((1,), (1,)), ((), ())),
        precision=lax.Precision.HIGH,
        preferred_element_type=jnp.float32,
    )


def lookup(source, indices, first_row):
    position = indices - first_row
    inside = (position >= 0) & (position < source.shape[0])
    picked = jnp.take(source, jnp.clip(position, 0, source.shape[0] - 1), axis=0)
    return jnp.where(inside[:, None], picked, 0.0)


def col_of(y, z):
    return (y % N_Y) * N_Z + z


def y_shift(value, step):
    pairs = [(col_of(y, z), col_of(y + step, z)) for y in range(N_Y) for z in range(N_Z)]
    return lax.ppermute(value, "col", pairs)


def pair_split(value, low):
    halves = value.reshape(2, value.shape[0] // 2, *value.shape[1:])
    return jnp.where(low, halves[0], halves[1]), jnp.where(low, halves[1], halves[0])


def pair_join(mine, other, low):
    return jnp.where(low, jnp.concatenate([mine, other]), jnp.concatenate([other, mine]))


def group_masked_sum(value):
    here = lax.axis_index("col")
    y, z = here // N_Z, here % N_Z
    zl = lax.axis_index("zl")
    quarter = value.shape[0] // N_Y

    def part(k):
        return lax.dynamic_slice_in_dim(value, ((y + k) % N_Y) * quarter, quarter)

    own = part(0)
    for k in range(1, N_Y):
        own = own + y_shift(part(k), k)
    zl_swap = [(0, 1), (1, 0)]
    z_swap = [(c, c ^ 1) for c in range(N_Y * N_Z)]
    mine, theirs = pair_split(own, zl == 0)
    mine = mine + lax.ppermute(theirs, "zl", zl_swap)
    low, high = pair_split(mine, z == 0)
    low = low + lax.ppermute(high, "col", z_swap)
    mine = pair_join(low, lax.ppermute(low, "col", z_swap), z == 0)
    own = pair_join(mine, lax.ppermute(mine, "zl", zl_swap), zl == 0)
    pieces = [own] + [y_shift(own, -k) for k in range(1, N_Y)]
    return jnp.roll(jnp.stack(pieces), y, axis=0).reshape(value.shape)


def all_max(value, axis, n):
    bit = 1
    while bit < n:
        value = jnp.maximum(value, lax.ppermute(value, axis, [(i, i ^ bit) for i in range(n)]))
        bit *= 2
    return value


def gather_in_order(parts, axis, n):
    here = lax.axis_index(axis)
    bit = 1
    while bit < n:
        other = lax.ppermute(parts, axis, [(i, i ^ bit) for i in range(n)])
        low = (here & bit) == 0
        parts = jnp.where(low, jnp.concatenate([parts, other]), jnp.concatenate([other, parts]))
        bit *= 2
    return parts


def x_shift(value, step, n_x):
    pairs = [(i, ((i // 2 + step) % n_x) * 2 + i % 2) for i in range(2 * n_x)]
    return lax.ppermute(value, "xc", pairs)


def xc_gather(shard, n_x):
    die = [(i, i ^ 1) for i in range(2 * n_x)]
    rows = shard.shape[0] // 2
    from_below = x_shift(shard, 1, n_x)
    from_above = x_shift(shard, -1, n_x)
    other = lax.ppermute(shard, "xc", die)
    far_low = x_shift(from_below[:rows], 1, n_x)
    far_high = x_shift(from_above[rows:], -1, n_x)
    near = lax.ppermute(jnp.stack([from_above, from_below]), "xc", die)
    other_far_low = lax.ppermute(far_low, "xc", die)
    other_far_high = lax.ppermute(far_high, "xc", die)
    return jnp.concatenate(
        [shard, other, from_above, near[0], far_low, far_high, other_far_low, other_far_high, from_below, near[1]]
    )


def body(slab_embed, coverage_old, sel_index, cand_index):
    n_xc = 8
    col_id = lax.axis_index("col")
    zl = lax.axis_index("zl")
    n_x = n_xc // 2
    x = lax.axis_index("xc") // 2
    core = lax.axis_index("xc") % 2
    shard_rows = slab_embed.shape[0]
    half = xc_gather(slab_embed, n_x)
    first_row = (col_id * 2 + zl) * half.shape[0]

    def to_local(index):
        canonical = index - first_row
        source = jnp.clip(canonical, 0, half.shape[0] - 1) // shard_rows
        offset = (source // 2 - x) % n_x
        return jnp.where(
            (canonical >= 0) & (canonical < half.shape[0]),
            (offset * 2 + (source % 2 ^ core)) * shard_rows + canonical % shard_rows,
            -1,
        )

    def to_canonical(value):
        parts = value.reshape(n_x, 2, -1)
        parts = jnp.where(core == 0, parts, parts[:, ::-1])
        return jnp.roll(parts, x, axis=0).reshape(-1)

    def to_relative(value):
        parts = jnp.roll(value.reshape(n_x, 2, -1), -x, axis=0)
        return jnp.where(core == 0, parts, parts[:, ::-1]).reshape(-1)

    zl_swap = [(0, 1), (1, 0)]
    both_sel = pair_join(sel_index, lax.ppermute(sel_index, "zl", zl_swap), zl == 0)
    both_cand = pair_join(cand_index, lax.ppermute(cand_index, "zl", zl_swap), zl == 0)
    selected = group_masked_sum(lookup(half, to_local(both_sel), 0))
    chosen = group_masked_sum(lookup(half, to_local(both_cand), 0))
    n_sel = both_sel.shape[0]
    scores = lax.optimization_barrier(similar(jnp.concatenate([selected, chosen]), half))
    partial = to_canonical(jnp.max(scores[:n_sel], axis=0))
    reached = all_max(partial, "xc", n_xc)
    old = lax.dynamic_slice_in_dim(coverage_old, zl * half.shape[0], half.shape[0])
    coverage = jnp.maximum(old, reached)
    local_coverage = to_relative(coverage)
    gain_part = jnp.sum(jnp.maximum(scores[n_sel:] - local_coverage[None, :], 0.0), axis=1)
    parts = gather_in_order(gather_in_order(gain_part[None], "zl", 2)[None], "col", N_Y * N_Z)
    total = jnp.sum(parts.reshape(-1, gain_part.shape[0]), axis=0)
    total_gain = lax.dynamic_slice_in_dim(total, zl * cand_index.shape[0], cand_index.shape[0])
    full_coverage = pair_join(coverage, lax.ppermute(coverage, "zl", zl_swap), zl == 0)
    return (full_coverage, total_gain)


def solution(mesh):
    shape = dict(zip(mesh.axis_names, mesh.devices.shape))
    names, sizes = [], []
    for name in mesh.axis_names:
        if name == "row":
            names += ["zl", "xc"]
            sizes += [2, shape["row"] // 2]
        else:
            names.append(name)
            sizes.append(shape[name])
    split = Mesh(mesh.devices.reshape(sizes), tuple(names))
    in_specs = (P(("col", "zl", "xc"), None), P("col"), P(("zl", "xc")), P(("zl", "xc")))
    out_specs = (P("col"), P(("zl", "xc")))
    return jax.shard_map(body, mesh=split, in_specs=in_specs, out_specs=out_specs, check_vma=False)
```

```python
import jax
import jax.numpy as jnp
from jax import lax
from jax.sharding import Mesh
from jax.sharding import PartitionSpec as P

N_Y, N_Z = 4, 2


def similar(left, right):
    return lax.dot_general(
        left,
        right,
        (((1,), (1,)), ((), ())),
        precision=lax.Precision.HIGH,
        preferred_element_type=jnp.float32,
    )


def lookup(source, indices, first_row):
    position = indices - first_row
    inside = (position >= 0) & (position < source.shape[0])
    picked = jnp.take(source, jnp.clip(position, 0, source.shape[0] - 1), axis=0)
    return jnp.where(inside[:, None], picked, 0.0)


def col_of(y, z):
    return (y % N_Y) * N_Z + z


def y_shift(value, step):
    pairs = [(col_of(y, z), col_of(y + step, z)) for y in range(N_Y) for z in range(N_Z)]
    return lax.ppermute(value, "col", pairs)


def pair_split(value, low):
    halves = value.reshape(2, value.shape[0] // 2, *value.shape[1:])
    return jnp.where(low, halves[0], halves[1]), jnp.where(low, halves[1], halves[0])


def pair_join(mine, other, low):
    return jnp.where(low, jnp.concatenate([mine, other]), jnp.concatenate([other, mine]))


def group_masked_sum(value):
    here = lax.axis_index("col")
    y, z = here // N_Z, here % N_Z
    zl = lax.axis_index("zl")
    quarter = value.shape[0] // N_Y

    def part(k):
        return lax.dynamic_slice_in_dim(value, ((y + k) % N_Y) * quarter, quarter)

    own = part(0)
    for k in range(1, N_Y):
        own = own + y_shift(part(k), k)
    zl_swap = [(0, 1), (1, 0)]
    z_swap = [(c, c ^ 1) for c in range(N_Y * N_Z)]
    mine, theirs = pair_split(own, zl == 0)
    mine = mine + lax.ppermute(theirs, "zl", zl_swap)
    low, high = pair_split(mine, z == 0)
    low = low + lax.ppermute(high, "col", z_swap)
    mine = pair_join(low, lax.ppermute(low, "col", z_swap), z == 0)
    own = pair_join(mine, lax.ppermute(mine, "zl", zl_swap), zl == 0)
    pieces = [own] + [y_shift(own, -k) for k in range(1, N_Y)]
    return jnp.roll(jnp.stack(pieces), y, axis=0).reshape(value.shape)


def group_masked_sum_z_first(value):
    here = lax.axis_index("col")
    y, z = here // N_Z, here % N_Z
    zl = lax.axis_index("zl")
    zl_swap = [(0, 1), (1, 0)]
    z_swap = [(c, c ^ 1) for c in range(N_Y * N_Z)]
    mine, theirs = pair_split(value, zl == 0)
    mine = mine + lax.ppermute(theirs, "zl", zl_swap)
    low, high = pair_split(mine, z == 0)
    low = low + lax.ppermute(high, "col", z_swap)
    quarter = low.shape[0] // N_Y

    def part(k):
        return lax.dynamic_slice_in_dim(low, ((y + k) % N_Y) * quarter, quarter)

    own = part(0)
    for k in range(1, N_Y):
        own = own + y_shift(part(k), k)
    pieces = [own] + [y_shift(own, -k) for k in range(1, N_Y)]
    low = jnp.roll(jnp.stack(pieces), y, axis=0).reshape(low.shape)
    mine = pair_join(low, lax.ppermute(low, "col", z_swap), z == 0)
    return pair_join(mine, lax.ppermute(mine, "zl", zl_swap), zl == 0)


def all_max(value, axis, n):
    bit = 1
    while bit < n:
        value = jnp.maximum(value, lax.ppermute(value, axis, [(i, i ^ bit) for i in range(n)]))
        bit *= 2
    return value


def gather_in_order(parts, axis, n):
    here = lax.axis_index(axis)
    bit = 1
    while bit < n:
        other = lax.ppermute(parts, axis, [(i, i ^ bit) for i in range(n)])
        low = (here & bit) == 0
        parts = jnp.where(low, jnp.concatenate([parts, other]), jnp.concatenate([other, parts]))
        bit *= 2
    return parts


def body(slab_embed, coverage_old, sel_index, cand_index):
    n_xc = 8
    col_id = lax.axis_index("col")
    zl = lax.axis_index("zl")
    half = lax.all_gather(slab_embed, "xc", axis=0, tiled=True)
    first_row = (col_id * 2 + zl) * half.shape[0]
    zl_swap = [(0, 1), (1, 0)]
    both_sel = pair_join(sel_index, lax.ppermute(sel_index, "zl", zl_swap), zl == 0)
    both_cand = pair_join(cand_index, lax.ppermute(cand_index, "zl", zl_swap), zl == 0)
    selected = group_masked_sum(lookup(half, both_sel, first_row))
    chosen = group_masked_sum_z_first(lookup(half, both_cand, first_row))
    n_sel = both_sel.shape[0]
    scores = lax.optimization_barrier(similar(jnp.concatenate([selected, chosen]), half))
    reached = all_max(jnp.max(scores[:n_sel], axis=0), "xc", n_xc)
    old = lax.dynamic_slice_in_dim(coverage_old, zl * half.shape[0], half.shape[0])
    coverage = jnp.maximum(old, reached)
    gain_part = jnp.sum(jnp.maximum(scores[n_sel:] - coverage[None, :], 0.0), axis=1)
    parts = gather_in_order(gather_in_order(gain_part[None], "zl", 2)[None], "col", N_Y * N_Z)
    total = jnp.sum(parts.reshape(-1, gain_part.shape[0]), axis=0)
    total_gain = lax.dynamic_slice_in_dim(total, zl * cand_index.shape[0], cand_index.shape[0])
    full_coverage = pair_join(coverage, lax.ppermute(coverage, "zl", zl_swap), zl == 0)
    return (full_coverage, total_gain)


def solution(mesh):
    shape = dict(zip(mesh.axis_names, mesh.devices.shape))
    names, sizes = [], []
    for name in mesh.axis_names:
        if name == "row":
            names += ["zl", "xc"]
            sizes += [2, shape["row"] // 2]
        else:
            names.append(name)
            sizes.append(shape[name])
    split = Mesh(mesh.devices.reshape(sizes), tuple(names))
    in_specs = (P(("col", "zl", "xc"), None), P("col"), P(("zl", "xc")), P(("zl", "xc")))
    out_specs = (P("col"), P(("zl", "xc")))
    return jax.shard_map(body, mesh=split, in_specs=in_specs, out_specs=out_specs, check_vma=False)
```

```python
import jax
import jax.numpy as jnp
from jax import lax
from jax.sharding import Mesh
from jax.sharding import PartitionSpec as P

N_Y, N_Z = 4, 2


def similar(left, right):
    return lax.dot_general(
        left,
        right,
        (((1,), (1,)), ((), ())),
        precision=lax.Precision.HIGH,
        preferred_element_type=jnp.float32,
    )


def lookup(source, indices, first_row):
    position = indices - first_row
    inside = (position >= 0) & (position < source.shape[0])
    picked = jnp.take(source, jnp.clip(position, 0, source.shape[0] - 1), axis=0)
    return jnp.where(inside[:, None], picked, 0.0)


def col_of(y, z):
    return (y % N_Y) * N_Z + z


def y_shift(value, step):
    pairs = [(col_of(y, z), col_of(y + step, z)) for y in range(N_Y) for z in range(N_Z)]
    return lax.ppermute(value, "col", pairs)


def pair_split(value, low):
    halves = value.reshape(2, value.shape[0] // 2, *value.shape[1:])
    return jnp.where(low, halves[0], halves[1]), jnp.where(low, halves[1], halves[0])


def pair_join(mine, other, low):
    return jnp.where(low, jnp.concatenate([mine, other]), jnp.concatenate([other, mine]))


def group_masked_sum(value):
    here = lax.axis_index("col")
    y, z = here // N_Z, here % N_Z
    zl = lax.axis_index("zl")
    quarter = value.shape[0] // N_Y

    def part(k):
        return lax.dynamic_slice_in_dim(value, ((y + k) % N_Y) * quarter, quarter)

    own = part(0)
    for k in range(1, N_Y):
        own = own + y_shift(part(k), k)
    zl_swap = [(0, 1), (1, 0)]
    z_swap = [(c, c ^ 1) for c in range(N_Y * N_Z)]
    mine, theirs = pair_split(own, zl == 0)
    mine = mine + lax.ppermute(theirs, "zl", zl_swap)
    low, high = pair_split(mine, z == 0)
    low = low + lax.ppermute(high, "col", z_swap)
    mine = pair_join(low, lax.ppermute(low, "col", z_swap), z == 0)
    own = pair_join(mine, lax.ppermute(mine, "zl", zl_swap), zl == 0)
    pieces = [own] + [y_shift(own, -k) for k in range(1, N_Y)]
    return jnp.roll(jnp.stack(pieces), y, axis=0).reshape(value.shape)


def all_max(value, axis, n):
    bit = 1
    while bit < n:
        value = jnp.maximum(value, lax.ppermute(value, axis, [(i, i ^ bit) for i in range(n)]))
        bit *= 2
    return value


def gather_in_order(parts, axis, n):
    here = lax.axis_index(axis)
    bit = 1
    while bit < n:
        other = lax.ppermute(parts, axis, [(i, i ^ bit) for i in range(n)])
        low = (here & bit) == 0
        parts = jnp.where(low, jnp.concatenate([parts, other]), jnp.concatenate([other, parts]))
        bit *= 2
    return parts


def body(slab_embed, coverage_old, sel_index, cand_index):
    n_xc = 8
    col_id = lax.axis_index("col")
    zl = lax.axis_index("zl")
    half = lax.all_gather(slab_embed, "xc", axis=0, tiled=True)
    first_row = (col_id * 2 + zl) * half.shape[0]
    zl_swap = [(0, 1), (1, 0)]
    both_sel = pair_join(sel_index, lax.ppermute(sel_index, "zl", zl_swap), zl == 0)
    both_cand = pair_join(cand_index, lax.ppermute(cand_index, "zl", zl_swap), zl == 0)
    n_sel = both_sel.shape[0]
    picked = lookup(half, jnp.concatenate([both_sel, both_cand]), first_row)
    selected = group_masked_sum(picked[:n_sel])
    chosen = group_masked_sum(picked[n_sel:])
    scores = lax.optimization_barrier(similar(jnp.concatenate([selected, chosen]), half))
    reached = all_max(jnp.max(scores[:n_sel], axis=0), "xc", n_xc)
    old = lax.dynamic_slice_in_dim(coverage_old, zl * half.shape[0], half.shape[0])
    coverage = jnp.maximum(old, reached)
    gain_part = jnp.sum(jnp.maximum(scores[n_sel:] - coverage[None, :], 0.0), axis=1)
    parts = gather_in_order(gather_in_order(gain_part[None], "zl", 2)[None], "col", N_Y * N_Z)
    total = jnp.sum(parts.reshape(-1, gain_part.shape[0]), axis=0)
    total_gain = lax.dynamic_slice_in_dim(total, zl * cand_index.shape[0], cand_index.shape[0])
    full_coverage = pair_join(coverage, lax.ppermute(coverage, "zl", zl_swap), zl == 0)
    return (full_coverage, total_gain)


def solution(mesh):
    shape = dict(zip(mesh.axis_names, mesh.devices.shape))
    names, sizes = [], []
    for name in mesh.axis_names:
        if name == "row":
            names += ["zl", "xc"]
            sizes += [2, shape["row"] // 2]
        else:
            names.append(name)
            sizes.append(shape[name])
    split = Mesh(mesh.devices.reshape(sizes), tuple(names))
    in_specs = (P(("col", "zl", "xc"), None), P("col"), P(("zl", "xc")), P(("zl", "xc")))
    out_specs = (P("col"), P(("zl", "xc")))
    return jax.shard_map(body, mesh=split, in_specs=in_specs, out_specs=out_specs, check_vma=False)
```

```python
import jax
import jax.numpy as jnp
from jax import lax
from jax.sharding import Mesh
from jax.sharding import PartitionSpec as P

N_Y, N_Z = 4, 2


def similar(left, right):
    return lax.dot_general(
        left,
        right,
        (((1,), (1,)), ((), ())),
        precision=lax.Precision.HIGH,
        preferred_element_type=jnp.float32,
    )


def lookup(source, indices, first_row):
    position = indices - first_row
    inside = (position >= 0) & (position < source.shape[0])
    picked = jnp.take(source, jnp.clip(position, 0, source.shape[0] - 1), axis=0)
    return jnp.where(inside[:, None], picked, 0.0)


def col_of(y, z):
    return (y % N_Y) * N_Z + z


def y_shift(value, step):
    pairs = [(col_of(y, z), col_of(y + step, z)) for y in range(N_Y) for z in range(N_Z)]
    return lax.ppermute(value, "col", pairs)


def pair_split(value, low):
    halves = value.reshape(2, value.shape[0] // 2, *value.shape[1:])
    return jnp.where(low, halves[0], halves[1]), jnp.where(low, halves[1], halves[0])


def pair_join(mine, other, low):
    return jnp.where(low, jnp.concatenate([mine, other]), jnp.concatenate([other, mine]))


def group_masked_sum(value):
    here = lax.axis_index("col")
    y, z = here // N_Z, here % N_Z
    zl = lax.axis_index("zl")
    quarter = value.shape[0] // N_Y

    def part(k):
        return lax.dynamic_slice_in_dim(value, ((y + k) % N_Y) * quarter, quarter)

    own = part(0)
    for k in range(1, N_Y):
        own = own + y_shift(part(k), k)
    zl_swap = [(0, 1), (1, 0)]
    z_swap = [(c, c ^ 1) for c in range(N_Y * N_Z)]
    mine, theirs = pair_split(own, zl == 0)
    mine = mine + lax.ppermute(theirs, "zl", zl_swap)
    low, high = pair_split(mine, z == 0)
    low = low + lax.ppermute(high, "col", z_swap)
    mine = pair_join(low, lax.ppermute(low, "col", z_swap), z == 0)
    own = pair_join(mine, lax.ppermute(mine, "zl", zl_swap), zl == 0)
    pieces = [own] + [y_shift(own, -k) for k in range(1, N_Y)]
    return jnp.roll(jnp.stack(pieces), y, axis=0).reshape(value.shape)


def all_max(value, axis, n):
    bit = 1
    while bit < n:
        value = jnp.maximum(value, lax.ppermute(value, axis, [(i, i ^ bit) for i in range(n)]))
        bit *= 2
    return value


def gather_in_order(parts, axis, n):
    here = lax.axis_index(axis)
    bit = 1
    while bit < n:
        other = lax.ppermute(parts, axis, [(i, i ^ bit) for i in range(n)])
        low = (here & bit) == 0
        parts = jnp.where(low, jnp.concatenate([parts, other]), jnp.concatenate([other, parts]))
        bit *= 2
    return parts


def body(slab_embed, coverage_old, sel_index, cand_index):
    n_xc = 8
    col_id = lax.axis_index("col")
    zl = lax.axis_index("zl")
    half = lax.all_gather(slab_embed, "xc", axis=0, tiled=True)
    first_row = (col_id * 2 + zl) * half.shape[0]
    zl_swap = [(0, 1), (1, 0)]
    both_sel = pair_join(sel_index, lax.ppermute(sel_index, "zl", zl_swap), zl == 0)
    both_cand = pair_join(cand_index, lax.ppermute(cand_index, "zl", zl_swap), zl == 0)
    selected = group_masked_sum(lookup(half, both_sel, first_row))
    selected, cand_rows = lax.optimization_barrier((selected, lookup(half, both_cand, first_row)))
    chosen = group_masked_sum(cand_rows)
    reached = all_max(jnp.max(similar(selected, half), axis=0), "xc", n_xc)
    old = lax.dynamic_slice_in_dim(coverage_old, zl * half.shape[0], half.shape[0])
    coverage = jnp.maximum(old, reached)
    scores = lax.optimization_barrier(similar(chosen, half))
    gain_part = jnp.sum(jnp.maximum(scores - coverage[None, :], 0.0), axis=1)
    parts = gather_in_order(gather_in_order(gain_part[None], "zl", 2)[None], "col", N_Y * N_Z)
    total = jnp.sum(parts.reshape(-1, gain_part.shape[0]), axis=0)
    total_gain = lax.dynamic_slice_in_dim(total, zl * cand_index.shape[0], cand_index.shape[0])
    full_coverage = pair_join(coverage, lax.ppermute(coverage, "zl", zl_swap), zl == 0)
    return (full_coverage, total_gain)


def solution(mesh):
    shape = dict(zip(mesh.axis_names, mesh.devices.shape))
    names, sizes = [], []
    for name in mesh.axis_names:
        if name == "row":
            names += ["zl", "xc"]
            sizes += [2, shape["row"] // 2]
        else:
            names.append(name)
            sizes.append(shape[name])
    split = Mesh(mesh.devices.reshape(sizes), tuple(names))
    in_specs = (P(("col", "zl", "xc"), None), P("col"), P(("zl", "xc")), P(("zl", "xc")))
    out_specs = (P("col"), P(("zl", "xc")))
    return jax.shard_map(body, mesh=split, in_specs=in_specs, out_specs=out_specs, check_vma=False)
```

```python
import jax
import jax.numpy as jnp
from jax import lax
from jax.sharding import Mesh
from jax.sharding import PartitionSpec as P

N_Y, N_Z = 4, 2


def similar(left, right):
    return lax.dot_general(
        left,
        right,
        (((1,), (1,)), ((), ())),
        precision=lax.Precision.HIGH,
        preferred_element_type=jnp.float32,
    )


def lookup(source, indices, first_row):
    position = indices - first_row
    inside = (position >= 0) & (position < source.shape[0])
    picked = jnp.take(source, jnp.clip(position, 0, source.shape[0] - 1), axis=0)
    return jnp.where(inside[:, None], picked, 0.0)


def col_of(y, z):
    return (y % N_Y) * N_Z + z


def y_shift(value, step):
    pairs = [(col_of(y, z), col_of(y + step, z)) for y in range(N_Y) for z in range(N_Z)]
    return lax.ppermute(value, "col", pairs)


def pair_split(value, low):
    halves = value.reshape(2, value.shape[0] // 2, *value.shape[1:])
    return jnp.where(low, halves[0], halves[1]), jnp.where(low, halves[1], halves[0])


def pair_join(mine, other, low):
    return jnp.where(low, jnp.concatenate([mine, other]), jnp.concatenate([other, mine]))


def z_group_shift(value, k):
    if k == 1:
        return lax.ppermute(value, "col", [(c, c ^ 1) for c in range(N_Y * N_Z)])
    if k == 2:
        return lax.ppermute(value, "zl", [(0, 1), (1, 0)])
    n = 2 * N_Y * N_Z
    return lax.ppermute(value, ("zl", "col"), [(i, i ^ (N_Y * N_Z) ^ 1) for i in range(n)])


def group_masked_sum(value):
    here = lax.axis_index("col")
    y, z = here // N_Z, here % N_Z
    g = lax.axis_index("zl") * 2 + z
    quarter = value.shape[0] // N_Y

    def part(k):
        return lax.dynamic_slice_in_dim(value, ((y + k) % N_Y) * quarter, quarter)

    own = part(0)
    for k in range(1, N_Y):
        own = own + y_shift(part(k), k)
    piece = quarter // 4

    def z_part(k):
        return lax.dynamic_slice_in_dim(own, (g ^ k) * piece, piece)

    mine = z_part(0)
    for k in range(1, 4):
        mine = mine + z_group_shift(z_part(k), k)
    received = jnp.stack([mine] + [z_group_shift(mine, k) for k in range(1, 4)])
    own = jnp.take(received, jnp.arange(4) ^ g, axis=0).reshape(own.shape)
    pieces = [own] + [y_shift(own, -k) for k in range(1, N_Y)]
    return jnp.roll(jnp.stack(pieces), y, axis=0).reshape(value.shape)


def all_max(value, axis, n):
    bit = 1
    while bit < n:
        value = jnp.maximum(value, lax.ppermute(value, axis, [(i, i ^ bit) for i in range(n)]))
        bit *= 2
    return value


def gather_in_order(parts, axis, n):
    here = lax.axis_index(axis)
    bit = 1
    while bit < n:
        other = lax.ppermute(parts, axis, [(i, i ^ bit) for i in range(n)])
        low = (here & bit) == 0
        parts = jnp.where(low, jnp.concatenate([parts, other]), jnp.concatenate([other, parts]))
        bit *= 2
    return parts


def body(slab_embed, coverage_old, sel_index, cand_index):
    n_xc = 8
    col_id = lax.axis_index("col")
    zl = lax.axis_index("zl")
    half = lax.all_gather(slab_embed, "xc", axis=0, tiled=True)
    first_row = (col_id * 2 + zl) * half.shape[0]
    zl_swap = [(0, 1), (1, 0)]
    both_sel = pair_join(sel_index, lax.ppermute(sel_index, "zl", zl_swap), zl == 0)
    both_cand = pair_join(cand_index, lax.ppermute(cand_index, "zl", zl_swap), zl == 0)
    selected = group_masked_sum(lookup(half, both_sel, first_row))
    chosen = group_masked_sum(lookup(half, both_cand, first_row))
    n_sel = both_sel.shape[0]
    scores = lax.optimization_barrier(similar(jnp.concatenate([selected, chosen]), half))
    reached = all_max(jnp.max(scores[:n_sel], axis=0), "xc", n_xc)
    old = lax.dynamic_slice_in_dim(coverage_old, zl * half.shape[0], half.shape[0])
    coverage = jnp.maximum(old, reached)
    gain_part = jnp.sum(jnp.maximum(scores[n_sel:] - coverage[None, :], 0.0), axis=1)
    parts = gather_in_order(gather_in_order(gain_part[None], "zl", 2)[None], "col", N_Y * N_Z)
    total = jnp.sum(parts.reshape(-1, gain_part.shape[0]), axis=0)
    total_gain = lax.dynamic_slice_in_dim(total, zl * cand_index.shape[0], cand_index.shape[0])
    full_coverage = pair_join(coverage, lax.ppermute(coverage, "zl", zl_swap), zl == 0)
    return (full_coverage, total_gain)


def solution(mesh):
    shape = dict(zip(mesh.axis_names, mesh.devices.shape))
    names, sizes = [], []
    for name in mesh.axis_names:
        if name == "row":
            names += ["zl", "xc"]
            sizes += [2, shape["row"] // 2]
        else:
            names.append(name)
            sizes.append(shape[name])
    split = Mesh(mesh.devices.reshape(sizes), tuple(names))
    in_specs = (P(("col", "zl", "xc"), None), P("col"), P(("zl", "xc")), P(("zl", "xc")))
    out_specs = (P("col"), P(("zl", "xc")))
    return jax.shard_map(body, mesh=split, in_specs=in_specs, out_specs=out_specs, check_vma=False)
```

```python
import jax
import jax.numpy as jnp
from jax import lax
from jax.sharding import Mesh
from jax.sharding import PartitionSpec as P

N_Y, N_Z = 4, 2


def similar(left, right):
    return lax.dot_general(
        left,
        right,
        (((1,), (1,)), ((), ())),
        precision=lax.Precision.HIGH,
        preferred_element_type=jnp.float32,
    )


def lookup(source, indices, first_row):
    position = indices - first_row
    inside = (position >= 0) & (position < source.shape[0])
    picked = jnp.take(source, jnp.clip(position, 0, source.shape[0] - 1), axis=0)
    return jnp.where(inside[:, None], picked, 0.0)


def col_of(y, z):
    return (y % N_Y) * N_Z + z


def y_shift(value, step):
    pairs = [(col_of(y, z), col_of(y + step, z)) for y in range(N_Y) for z in range(N_Z)]
    return lax.ppermute(value, "col", pairs)


def pair_split(value, low):
    halves = value.reshape(2, value.shape[0] // 2, *value.shape[1:])
    return jnp.where(low, halves[0], halves[1]), jnp.where(low, halves[1], halves[0])


def pair_join(mine, other, low):
    return jnp.where(low, jnp.concatenate([mine, other]), jnp.concatenate([other, mine]))


def z_group_shift(value, k):
    if k == 1:
        return lax.ppermute(value, "col", [(c, c ^ 1) for c in range(N_Y * N_Z)])
    if k == 2:
        return lax.ppermute(value, "zl", [(0, 1), (1, 0)])
    n = 2 * N_Y * N_Z
    return lax.ppermute(value, ("zl", "col"), [(i, i ^ (N_Y * N_Z) ^ 1) for i in range(n)])


def group_masked_sum(value):
    here = lax.axis_index("col")
    y, z = here // N_Z, here % N_Z
    g = lax.axis_index("zl") * 2 + z
    quarter = value.shape[0] // N_Y

    def part(k):
        return lax.dynamic_slice_in_dim(value, ((y + k) % N_Y) * quarter, quarter)

    own = part(0)
    for k in range(1, N_Y):
        own = own + y_shift(part(k), k)
    piece = quarter // 4

    def z_part(k):
        return lax.dynamic_slice_in_dim(own, (g ^ k) * piece, piece)

    mine = z_part(0)
    for k in range(1, 4):
        mine = mine + z_group_shift(z_part(k), k)
    received = jnp.stack([mine] + [z_group_shift(mine, k) for k in range(1, 4)])
    own = jnp.take(received, jnp.arange(4) ^ g, axis=0).reshape(own.shape)
    pieces = [own] + [y_shift(own, -k) for k in range(1, N_Y)]
    return jnp.roll(jnp.stack(pieces), y, axis=0).reshape(value.shape)


def all_max_two_rounds(value, axis, n):
    for bits in ((1, 2, 3), (4,)):
        received = [lax.ppermute(value, axis, [(i, i ^ k) for i in range(n)]) for k in bits]
        for other in received:
            value = jnp.maximum(value, other)
    return value


def group_gather_in_order(value):
    here = lax.axis_index("col")
    y, z = here // N_Z, here % N_Z
    g = lax.axis_index("zl") * 2 + z
    received = jnp.stack([value] + [z_group_shift(value, k) for k in range(1, 4)])
    z_ordered = jnp.take(received, jnp.arange(4) ^ g, axis=0)
    col_pairs = [[(c, c ^ (2 * k)) for c in range(N_Y * N_Z)] for k in range(1, N_Y)]
    received = jnp.stack([z_ordered] + [lax.ppermute(z_ordered, "col", pairs) for pairs in col_pairs])
    return jnp.take(received, jnp.arange(N_Y) ^ y, axis=0)


def all_max(value, axis, n):
    bit = 1
    while bit < n:
        value = jnp.maximum(value, lax.ppermute(value, axis, [(i, i ^ bit) for i in range(n)]))
        bit *= 2
    return value


def gather_in_order(parts, axis, n):
    here = lax.axis_index(axis)
    bit = 1
    while bit < n:
        other = lax.ppermute(parts, axis, [(i, i ^ bit) for i in range(n)])
        low = (here & bit) == 0
        parts = jnp.where(low, jnp.concatenate([parts, other]), jnp.concatenate([other, parts]))
        bit *= 2
    return parts


def body(slab_embed, coverage_old, sel_index, cand_index):
    n_xc = 8
    col_id = lax.axis_index("col")
    zl = lax.axis_index("zl")
    half = lax.all_gather(slab_embed, "xc", axis=0, tiled=True)
    first_row = (col_id * 2 + zl) * half.shape[0]
    zl_swap = [(0, 1), (1, 0)]
    both_sel = pair_join(sel_index, lax.ppermute(sel_index, "zl", zl_swap), zl == 0)
    both_cand = pair_join(cand_index, lax.ppermute(cand_index, "zl", zl_swap), zl == 0)
    selected = group_masked_sum(lookup(half, both_sel, first_row))
    chosen = group_masked_sum(lookup(half, both_cand, first_row))
    n_sel = both_sel.shape[0]
    scores = lax.optimization_barrier(similar(jnp.concatenate([selected, chosen]), half))
    reached = all_max_two_rounds(jnp.max(scores[:n_sel], axis=0), "xc", n_xc)
    old = lax.dynamic_slice_in_dim(coverage_old, zl * half.shape[0], half.shape[0])
    coverage = jnp.maximum(old, reached)
    gain_part = jnp.sum(jnp.maximum(scores[n_sel:] - coverage[None, :], 0.0), axis=1)
    parts = group_gather_in_order(gain_part)
    total = jnp.sum(parts.reshape(-1, gain_part.shape[0]), axis=0)
    total_gain = lax.dynamic_slice_in_dim(total, zl * cand_index.shape[0], cand_index.shape[0])
    full_coverage = pair_join(coverage, lax.ppermute(coverage, "zl", zl_swap), zl == 0)
    return (full_coverage, total_gain)


def solution(mesh):
    shape = dict(zip(mesh.axis_names, mesh.devices.shape))
    names, sizes = [], []
    for name in mesh.axis_names:
        if name == "row":
            names += ["zl", "xc"]
            sizes += [2, shape["row"] // 2]
        else:
            names.append(name)
            sizes.append(shape[name])
    split = Mesh(mesh.devices.reshape(sizes), tuple(names))
    in_specs = (P(("col", "zl", "xc"), None), P("col"), P(("zl", "xc")), P(("zl", "xc")))
    out_specs = (P("col"), P(("zl", "xc")))
    return jax.shard_map(body, mesh=split, in_specs=in_specs, out_specs=out_specs, check_vma=False)
```

```python
import jax
import jax.numpy as jnp
from jax import lax
from jax.sharding import Mesh
from jax.sharding import PartitionSpec as P

N_Y, N_Z = 4, 2


def similar(left, right):
    return lax.dot_general(
        left,
        right,
        (((1,), (1,)), ((), ())),
        precision=lax.Precision.HIGH,
        preferred_element_type=jnp.float32,
    )


def lookup(source, indices, first_row):
    position = indices - first_row
    inside = (position >= 0) & (position < source.shape[0])
    picked = jnp.take(source, jnp.clip(position, 0, source.shape[0] - 1), axis=0)
    return jnp.where(inside[:, None], picked, 0.0)


def col_of(y, z):
    return (y % N_Y) * N_Z + z


def y_shift(value, step):
    pairs = [(col_of(y, z), col_of(y + step, z)) for y in range(N_Y) for z in range(N_Z)]
    return lax.ppermute(value, "col", pairs)


def pair_split(value, low):
    halves = value.reshape(2, value.shape[0] // 2, *value.shape[1:])
    return jnp.where(low, halves[0], halves[1]), jnp.where(low, halves[1], halves[0])


def pair_join(mine, other, low):
    return jnp.where(low, jnp.concatenate([mine, other]), jnp.concatenate([other, mine]))


def z_group_shift(value, k):
    if k == 1:
        return lax.ppermute(value, "col", [(c, c ^ 1) for c in range(N_Y * N_Z)])
    if k == 2:
        return lax.ppermute(value, "zl", [(0, 1), (1, 0)])
    n = 2 * N_Y * N_Z
    return lax.ppermute(value, ("zl", "col"), [(i, i ^ (N_Y * N_Z) ^ 1) for i in range(n)])


def group_masked_sum(value):
    here = lax.axis_index("col")
    y, z = here // N_Z, here % N_Z
    g = lax.axis_index("zl") * 2 + z
    quarter = value.shape[0] // N_Y

    def part(k):
        return lax.dynamic_slice_in_dim(value, ((y + k) % N_Y) * quarter, quarter)

    own = part(0)
    for k in range(1, N_Y):
        own = own + y_shift(part(k), k)
    piece = quarter // 4

    def z_part(k):
        return lax.dynamic_slice_in_dim(own, (g ^ k) * piece, piece)

    mine = z_part(0)
    for k in range(1, 4):
        mine = mine + z_group_shift(z_part(k), k)
    received = jnp.stack([mine] + [z_group_shift(mine, k) for k in range(1, 4)])
    own = jnp.take(received, jnp.arange(4) ^ g, axis=0).reshape(own.shape)
    pieces = [own] + [y_shift(own, -k) for k in range(1, N_Y)]
    return jnp.roll(jnp.stack(pieces), y, axis=0).reshape(value.shape)


def all_max_two_rounds(value, axis, n):
    for bits in ((1, 2, 3), (4,)):
        received = [lax.ppermute(value, axis, [(i, i ^ k) for i in range(n)]) for k in bits]
        for other in received:
            value = jnp.maximum(value, other)
    return value


def group_gather_in_order(value):
    here = lax.axis_index("col")
    y, z = here // N_Z, here % N_Z
    g = lax.axis_index("zl") * 2 + z
    received = jnp.stack([value] + [z_group_shift(value, k) for k in range(1, 4)])
    z_ordered = jnp.take(received, jnp.arange(4) ^ g, axis=0)
    col_pairs = [[(c, c ^ (2 * k)) for c in range(N_Y * N_Z)] for k in range(1, N_Y)]
    received = jnp.stack([z_ordered] + [lax.ppermute(z_ordered, "col", pairs) for pairs in col_pairs])
    return jnp.take(received, jnp.arange(N_Y) ^ y, axis=0)


def all_max(value, axis, n):
    bit = 1
    while bit < n:
        value = jnp.maximum(value, lax.ppermute(value, axis, [(i, i ^ bit) for i in range(n)]))
        bit *= 2
    return value


def gather_in_order(parts, axis, n):
    here = lax.axis_index(axis)
    bit = 1
    while bit < n:
        other = lax.ppermute(parts, axis, [(i, i ^ bit) for i in range(n)])
        low = (here & bit) == 0
        parts = jnp.where(low, jnp.concatenate([parts, other]), jnp.concatenate([other, parts]))
        bit *= 2
    return parts


def body(slab_embed, coverage_old, sel_index, cand_index):
    n_xc = 8
    col_id = lax.axis_index("col")
    zl = lax.axis_index("zl")
    half = lax.all_gather(slab_embed, "xc", axis=0, tiled=True)
    first_row = (col_id * 2 + zl) * half.shape[0]
    zl_swap = [(0, 1), (1, 0)]
    both_sel = pair_join(sel_index, lax.ppermute(sel_index, "zl", zl_swap), zl == 0)
    both_cand = pair_join(cand_index, lax.ppermute(cand_index, "zl", zl_swap), zl == 0)
    selected = group_masked_sum(lookup(half, both_sel, first_row))
    chosen = group_masked_sum(lookup(half, both_cand, first_row))
    n_sel = both_sel.shape[0]
    sel_scores = lax.optimization_barrier(similar(selected, half))
    reached = all_max_two_rounds(jnp.max(sel_scores, axis=0), "xc", n_xc)
    old = lax.dynamic_slice_in_dim(coverage_old, zl * half.shape[0], half.shape[0])
    coverage = jnp.maximum(old, reached)
    gain_part = jnp.sum(jnp.maximum(similar(chosen, half) - coverage[None, :], 0.0), axis=1)
    parts = group_gather_in_order(gain_part)
    total = jnp.sum(parts.reshape(-1, gain_part.shape[0]), axis=0)
    total_gain = lax.dynamic_slice_in_dim(total, zl * cand_index.shape[0], cand_index.shape[0])
    full_coverage = pair_join(coverage, lax.ppermute(coverage, "zl", zl_swap), zl == 0)
    return (full_coverage, total_gain)


def solution(mesh):
    shape = dict(zip(mesh.axis_names, mesh.devices.shape))
    names, sizes = [], []
    for name in mesh.axis_names:
        if name == "row":
            names += ["zl", "xc"]
            sizes += [2, shape["row"] // 2]
        else:
            names.append(name)
            sizes.append(shape[name])
    split = Mesh(mesh.devices.reshape(sizes), tuple(names))
    in_specs = (P(("col", "zl", "xc"), None), P("col"), P(("zl", "xc")), P(("zl", "xc")))
    out_specs = (P("col"), P(("zl", "xc")))
    return jax.shard_map(body, mesh=split, in_specs=in_specs, out_specs=out_specs, check_vma=False)
```

```python
import jax
import jax.numpy as jnp
from jax import lax
from jax.sharding import Mesh
from jax.sharding import PartitionSpec as P

N_Y, N_Z = 4, 2


def similar(left, right):
    return lax.dot_general(
        left,
        right,
        (((1,), (1,)), ((), ())),
        precision=lax.Precision.HIGH,
        preferred_element_type=jnp.float32,
    )


def lookup(source, indices, first_row):
    position = indices - first_row
    inside = (position >= 0) & (position < source.shape[0])
    picked = jnp.take(source, jnp.clip(position, 0, source.shape[0] - 1), axis=0)
    return jnp.where(inside[:, None], picked, 0.0)


def col_of(y, z):
    return (y % N_Y) * N_Z + z


def y_shift(value, step):
    pairs = [(col_of(y, z), col_of(y + step, z)) for y in range(N_Y) for z in range(N_Z)]
    return lax.ppermute(value, "col", pairs)


def pair_split(value, low):
    halves = value.reshape(2, value.shape[0] // 2, *value.shape[1:])
    return jnp.where(low, halves[0], halves[1]), jnp.where(low, halves[1], halves[0])


def pair_join(mine, other, low):
    return jnp.where(low, jnp.concatenate([mine, other]), jnp.concatenate([other, mine]))


def z_group_shift(value, k):
    if k == 1:
        return lax.ppermute(value, "col", [(c, c ^ 1) for c in range(N_Y * N_Z)])
    if k == 2:
        return lax.ppermute(value, "zl", [(0, 1), (1, 0)])
    n = 2 * N_Y * N_Z
    return lax.ppermute(value, ("zl", "col"), [(i, i ^ (N_Y * N_Z) ^ 1) for i in range(n)])


def group_masked_sum(value):
    here = lax.axis_index("col")
    y, z = here // N_Z, here % N_Z
    g = lax.axis_index("zl") * 2 + z
    quarter = value.shape[0] // N_Y

    def part(k):
        return lax.dynamic_slice_in_dim(value, ((y + k) % N_Y) * quarter, quarter)

    own = part(0)
    for k in range(1, N_Y):
        own = own + y_shift(part(k), k)
    piece = quarter // 4

    def z_part(k):
        return lax.dynamic_slice_in_dim(own, (g ^ k) * piece, piece)

    mine = z_part(0)
    for k in range(1, 4):
        mine = mine + z_group_shift(z_part(k), k)
    received = jnp.stack([mine] + [z_group_shift(mine, k) for k in range(1, 4)])
    own = jnp.take(received, jnp.arange(4) ^ g, axis=0).reshape(own.shape)
    pieces = [own] + [y_shift(own, -k) for k in range(1, N_Y)]
    return jnp.roll(jnp.stack(pieces), y, axis=0).reshape(value.shape)


def all_max_two_rounds(value, axis, n):
    for bits in ((1, 2, 3), (4,)):
        received = [lax.ppermute(value, axis, [(i, i ^ k) for i in range(n)]) for k in bits]
        for other in received:
            value = jnp.maximum(value, other)
    return value


def group_gather_in_order(value):
    here = lax.axis_index("col")
    y, z = here // N_Z, here % N_Z
    g = lax.axis_index("zl") * 2 + z
    received = jnp.stack([value] + [z_group_shift(value, k) for k in range(1, 4)])
    z_ordered = jnp.take(received, jnp.arange(4) ^ g, axis=0)
    col_pairs = [[(c, c ^ (2 * k)) for c in range(N_Y * N_Z)] for k in range(1, N_Y)]
    received = jnp.stack([z_ordered] + [lax.ppermute(z_ordered, "col", pairs) for pairs in col_pairs])
    return jnp.take(received, jnp.arange(N_Y) ^ y, axis=0)


def all_max(value, axis, n):
    bit = 1
    while bit < n:
        value = jnp.maximum(value, lax.ppermute(value, axis, [(i, i ^ bit) for i in range(n)]))
        bit *= 2
    return value


def gather_in_order(parts, axis, n):
    here = lax.axis_index(axis)
    bit = 1
    while bit < n:
        other = lax.ppermute(parts, axis, [(i, i ^ bit) for i in range(n)])
        low = (here & bit) == 0
        parts = jnp.where(low, jnp.concatenate([parts, other]), jnp.concatenate([other, parts]))
        bit *= 2
    return parts


def body(slab_embed, coverage_old, sel_index, cand_index):
    n_xc = 8
    col_id = lax.axis_index("col")
    zl = lax.axis_index("zl")
    half = lax.all_gather(slab_embed, "xc", axis=0, tiled=True)
    first_row = (col_id * 2 + zl) * half.shape[0]
    zl_swap = [(0, 1), (1, 0)]
    both_sel = pair_join(sel_index, lax.ppermute(sel_index, "zl", zl_swap), zl == 0)
    both_cand = pair_join(cand_index, lax.ppermute(cand_index, "zl", zl_swap), zl == 0)
    cand_rows, sel_source = lax.optimization_barrier((lookup(half, both_cand, first_row), half))
    chosen = group_masked_sum(cand_rows)
    selected = group_masked_sum(lookup(sel_source, both_sel, first_row))
    n_sel = both_sel.shape[0]
    sel_scores = lax.optimization_barrier(similar(selected, half))
    reached = all_max_two_rounds(jnp.max(sel_scores, axis=0), "xc", n_xc)
    old = lax.dynamic_slice_in_dim(coverage_old, zl * half.shape[0], half.shape[0])
    coverage = jnp.maximum(old, reached)
    gain_part = jnp.sum(jnp.maximum(similar(chosen, half) - coverage[None, :], 0.0), axis=1)
    parts = group_gather_in_order(gain_part)
    total = jnp.sum(parts.reshape(-1, gain_part.shape[0]), axis=0)
    total_gain = lax.dynamic_slice_in_dim(total, zl * cand_index.shape[0], cand_index.shape[0])
    full_coverage = pair_join(coverage, lax.ppermute(coverage, "zl", zl_swap), zl == 0)
    return (full_coverage, total_gain)


def solution(mesh):
    shape = dict(zip(mesh.axis_names, mesh.devices.shape))
    names, sizes = [], []
    for name in mesh.axis_names:
        if name == "row":
            names += ["zl", "xc"]
            sizes += [2, shape["row"] // 2]
        else:
            names.append(name)
            sizes.append(shape[name])
    split = Mesh(mesh.devices.reshape(sizes), tuple(names))
    in_specs = (P(("col", "zl", "xc"), None), P("col"), P(("zl", "xc")), P(("zl", "xc")))
    out_specs = (P("col"), P(("zl", "xc")))
    return jax.shard_map(body, mesh=split, in_specs=in_specs, out_specs=out_specs, check_vma=False)
```

```python
import jax
import jax.numpy as jnp
from jax import lax
from jax.sharding import Mesh
from jax.sharding import PartitionSpec as P

N_Y, N_Z = 4, 2


def similar(left, right):
    return lax.dot_general(
        left,
        right,
        (((1,), (1,)), ((), ())),
        precision=lax.Precision.HIGH,
        preferred_element_type=jnp.float32,
    )


def lookup(source, indices, first_row):
    position = indices - first_row
    inside = (position >= 0) & (position < source.shape[0])
    picked = jnp.take(source, jnp.clip(position, 0, source.shape[0] - 1), axis=0)
    return jnp.where(inside[:, None], picked, 0.0)


def col_of(y, z):
    return (y % N_Y) * N_Z + z


def y_shift(value, step):
    pairs = [(col_of(y, z), col_of(y + step, z)) for y in range(N_Y) for z in range(N_Z)]
    return lax.ppermute(value, "col", pairs)


def pair_split(value, low):
    halves = value.reshape(2, value.shape[0] // 2, *value.shape[1:])
    return jnp.where(low, halves[0], halves[1]), jnp.where(low, halves[1], halves[0])


def pair_join(mine, other, low):
    return jnp.where(low, jnp.concatenate([mine, other]), jnp.concatenate([other, mine]))


def z_group_shift(value, k):
    if k == 1:
        return lax.ppermute(value, "col", [(c, c ^ 1) for c in range(N_Y * N_Z)])
    if k == 2:
        return lax.ppermute(value, "zl", [(0, 1), (1, 0)])
    n = 2 * N_Y * N_Z
    return lax.ppermute(value, ("zl", "col"), [(i, i ^ (N_Y * N_Z) ^ 1) for i in range(n)])


def group_masked_sum(value):
    here = lax.axis_index("col")
    y, z = here // N_Z, here % N_Z
    g = lax.axis_index("zl") * 2 + z
    quarter = value.shape[0] // N_Y

    def part(k):
        return lax.dynamic_slice_in_dim(value, ((y + k) % N_Y) * quarter, quarter)

    own = part(0)
    for k in range(1, N_Y):
        own = own + y_shift(part(k), k)
    piece = quarter // 4

    def z_part(k):
        return lax.dynamic_slice_in_dim(own, (g ^ k) * piece, piece)

    mine = z_part(0)
    for k in range(1, 4):
        mine = mine + z_group_shift(z_part(k), k)
    received = jnp.stack([mine] + [z_group_shift(mine, k) for k in range(1, 4)])
    own = jnp.take(received, jnp.arange(4) ^ g, axis=0).reshape(own.shape)
    pieces = [own] + [y_shift(own, -k) for k in range(1, N_Y)]
    return jnp.roll(jnp.stack(pieces), y, axis=0).reshape(value.shape)


def all_max_two_rounds(value, axis, n):
    for bits in ((1, 2, 3), (4,)):
        received = [lax.ppermute(value, axis, [(i, i ^ k) for i in range(n)]) for k in bits]
        for other in received:
            value = jnp.maximum(value, other)
    return value


def group_gather_in_order(value):
    here = lax.axis_index("col")
    y, z = here // N_Z, here % N_Z
    g = lax.axis_index("zl") * 2 + z
    received = jnp.stack([value] + [z_group_shift(value, k) for k in range(1, 4)])
    z_ordered = jnp.take(received, jnp.arange(4) ^ g, axis=0)
    col_pairs = [[(c, c ^ (2 * k)) for c in range(N_Y * N_Z)] for k in range(1, N_Y)]
    received = jnp.stack([z_ordered] + [lax.ppermute(z_ordered, "col", pairs) for pairs in col_pairs])
    return jnp.take(received, jnp.arange(N_Y) ^ y, axis=0)


def all_max(value, axis, n):
    bit = 1
    while bit < n:
        value = jnp.maximum(value, lax.ppermute(value, axis, [(i, i ^ bit) for i in range(n)]))
        bit *= 2
    return value


def gather_in_order(parts, axis, n):
    here = lax.axis_index(axis)
    bit = 1
    while bit < n:
        other = lax.ppermute(parts, axis, [(i, i ^ bit) for i in range(n)])
        low = (here & bit) == 0
        parts = jnp.where(low, jnp.concatenate([parts, other]), jnp.concatenate([other, parts]))
        bit *= 2
    return parts


def body(slab_embed, coverage_old, sel_index, cand_index):
    n_xc = 8
    col_id = lax.axis_index("col")
    zl = lax.axis_index("zl")
    half = lax.all_gather(slab_embed, "xc", axis=0, tiled=True)
    first_row = (col_id * 2 + zl) * half.shape[0]
    zl_swap = [(0, 1), (1, 0)]
    both_sel = pair_join(sel_index, lax.ppermute(sel_index, "zl", zl_swap), zl == 0)
    both_cand = pair_join(cand_index, lax.ppermute(cand_index, "zl", zl_swap), zl == 0)
    selected = group_masked_sum(lookup(half, both_sel, first_row))
    cand_rows = lookup(half, both_cand, first_row)
    split = cand_rows.shape[0] // 2
    chosen = jnp.concatenate([group_masked_sum(cand_rows[:split]), group_masked_sum(cand_rows[split:])])
    n_sel = both_sel.shape[0]
    sel_scores = lax.optimization_barrier(similar(selected, half))
    reached = all_max_two_rounds(jnp.max(sel_scores, axis=0), "xc", n_xc)
    old = lax.dynamic_slice_in_dim(coverage_old, zl * half.shape[0], half.shape[0])
    coverage = jnp.maximum(old, reached)
    gain_part = jnp.sum(jnp.maximum(similar(chosen, half) - coverage[None, :], 0.0), axis=1)
    parts = group_gather_in_order(gain_part)
    total = jnp.sum(parts.reshape(-1, gain_part.shape[0]), axis=0)
    total_gain = lax.dynamic_slice_in_dim(total, zl * cand_index.shape[0], cand_index.shape[0])
    full_coverage = pair_join(coverage, lax.ppermute(coverage, "zl", zl_swap), zl == 0)
    return (full_coverage, total_gain)


def solution(mesh):
    shape = dict(zip(mesh.axis_names, mesh.devices.shape))
    names, sizes = [], []
    for name in mesh.axis_names:
        if name == "row":
            names += ["zl", "xc"]
            sizes += [2, shape["row"] // 2]
        else:
            names.append(name)
            sizes.append(shape[name])
    split = Mesh(mesh.devices.reshape(sizes), tuple(names))
    in_specs = (P(("col", "zl", "xc"), None), P("col"), P(("zl", "xc")), P(("zl", "xc")))
    out_specs = (P("col"), P(("zl", "xc")))
    return jax.shard_map(body, mesh=split, in_specs=in_specs, out_specs=out_specs, check_vma=False)
```

```python
import jax
import jax.numpy as jnp
from jax import lax
from jax.sharding import Mesh
from jax.sharding import PartitionSpec as P

N_Y, N_Z = 4, 2


def similar(left, right):
    return lax.dot_general(
        left,
        right,
        (((1,), (1,)), ((), ())),
        precision=lax.Precision.HIGH,
        preferred_element_type=jnp.float32,
    )


def lookup(source, indices, first_row):
    position = indices - first_row
    inside = (position >= 0) & (position < source.shape[0])
    picked = jnp.take(source, jnp.clip(position, 0, source.shape[0] - 1), axis=0)
    return jnp.where(inside[:, None], picked, 0.0)


def col_of(y, z):
    return (y % N_Y) * N_Z + z


def y_shift(value, step):
    pairs = [(col_of(y, z), col_of(y + step, z)) for y in range(N_Y) for z in range(N_Z)]
    return lax.ppermute(value, "col", pairs)


def pair_split(value, low):
    halves = value.reshape(2, value.shape[0] // 2, *value.shape[1:])
    return jnp.where(low, halves[0], halves[1]), jnp.where(low, halves[1], halves[0])


def pair_join(mine, other, low):
    return jnp.where(low, jnp.concatenate([mine, other]), jnp.concatenate([other, mine]))


def z_group_shift(value, k):
    if k == 1:
        return lax.ppermute(value, "col", [(c, c ^ 1) for c in range(N_Y * N_Z)])
    if k == 2:
        return lax.ppermute(value, "zl", [(0, 1), (1, 0)])
    n = 2 * N_Y * N_Z
    return lax.ppermute(value, ("zl", "col"), [(i, i ^ (N_Y * N_Z) ^ 1) for i in range(n)])


def group_masked_sum(value):
    here = lax.axis_index("col")
    y, z = here // N_Z, here % N_Z
    g = lax.axis_index("zl") * 2 + z
    quarter = value.shape[0] // N_Y

    def part(k):
        return lax.dynamic_slice_in_dim(value, ((y + k) % N_Y) * quarter, quarter)

    own = part(0)
    for k in range(1, N_Y):
        own = own + y_shift(part(k), k)
    piece = quarter // 4

    def z_part(k):
        return lax.dynamic_slice_in_dim(own, (g ^ k) * piece, piece)

    mine = z_part(0)
    for k in range(1, 4):
        mine = mine + z_group_shift(z_part(k), k)
    received = jnp.stack([mine] + [z_group_shift(mine, k) for k in range(1, 4)])
    own = jnp.take(received, jnp.arange(4) ^ g, axis=0).reshape(own.shape)
    pieces = [own] + [y_shift(own, -k) for k in range(1, N_Y)]
    return jnp.roll(jnp.stack(pieces), y, axis=0).reshape(value.shape)


def all_max_two_rounds(value, axis, n):
    for bits in ((1, 2, 3), (4,)):
        received = [lax.ppermute(value, axis, [(i, i ^ k) for i in range(n)]) for k in bits]
        for other in received:
            value = jnp.maximum(value, other)
    return value


def group_gather_in_order(value):
    here = lax.axis_index("col")
    y, z = here // N_Z, here % N_Z
    g = lax.axis_index("zl") * 2 + z
    received = jnp.stack([value] + [z_group_shift(value, k) for k in range(1, 4)])
    z_ordered = jnp.take(received, jnp.arange(4) ^ g, axis=0)
    col_pairs = [[(c, c ^ (2 * k)) for c in range(N_Y * N_Z)] for k in range(1, N_Y)]
    received = jnp.stack([z_ordered] + [lax.ppermute(z_ordered, "col", pairs) for pairs in col_pairs])
    return jnp.take(received, jnp.arange(N_Y) ^ y, axis=0)


def all_max(value, axis, n):
    bit = 1
    while bit < n:
        value = jnp.maximum(value, lax.ppermute(value, axis, [(i, i ^ bit) for i in range(n)]))
        bit *= 2
    return value


def gather_in_order(parts, axis, n):
    here = lax.axis_index(axis)
    bit = 1
    while bit < n:
        other = lax.ppermute(parts, axis, [(i, i ^ bit) for i in range(n)])
        low = (here & bit) == 0
        parts = jnp.where(low, jnp.concatenate([parts, other]), jnp.concatenate([other, parts]))
        bit *= 2
    return parts


def body(slab_embed, coverage_old, sel_index, cand_index):
    n_xc = 8
    col_id = lax.axis_index("col")
    zl = lax.axis_index("zl")
    half = lax.all_gather(slab_embed, "xc", axis=0, tiled=True)
    first_row = (col_id * 2 + zl) * half.shape[0]
    zl_swap = [(0, 1), (1, 0)]
    both_sel = pair_join(sel_index, lax.ppermute(sel_index, "zl", zl_swap), zl == 0)
    both_cand = pair_join(cand_index, lax.ppermute(cand_index, "zl", zl_swap), zl == 0)
    selected = group_masked_sum(lookup(half, both_sel, first_row))
    chosen = group_masked_sum(lookup(half, both_cand, first_row))
    n_sel = both_sel.shape[0]
    width = half.shape[0] // 2
    sel_max = [
        jnp.max(lax.optimization_barrier(similar(selected, half[i * width:(i + 1) * width])), axis=0) for i in range(2)
    ]
    reached = all_max_two_rounds(jnp.concatenate(sel_max), "xc", n_xc)
    old = lax.dynamic_slice_in_dim(coverage_old, zl * half.shape[0], half.shape[0])
    coverage = jnp.maximum(old, reached)
    gain_part = jnp.sum(jnp.maximum(similar(chosen, half) - coverage[None, :], 0.0), axis=1)
    parts = group_gather_in_order(gain_part)
    total = jnp.sum(parts.reshape(-1, gain_part.shape[0]), axis=0)
    total_gain = lax.dynamic_slice_in_dim(total, zl * cand_index.shape[0], cand_index.shape[0])
    full_coverage = pair_join(coverage, lax.ppermute(coverage, "zl", zl_swap), zl == 0)
    return (full_coverage, total_gain)


def solution(mesh):
    shape = dict(zip(mesh.axis_names, mesh.devices.shape))
    names, sizes = [], []
    for name in mesh.axis_names:
        if name == "row":
            names += ["zl", "xc"]
            sizes += [2, shape["row"] // 2]
        else:
            names.append(name)
            sizes.append(shape[name])
    split = Mesh(mesh.devices.reshape(sizes), tuple(names))
    in_specs = (P(("col", "zl", "xc"), None), P("col"), P(("zl", "xc")), P(("zl", "xc")))
    out_specs = (P("col"), P(("zl", "xc")))
    return jax.shard_map(body, mesh=split, in_specs=in_specs, out_specs=out_specs, check_vma=False)
```

```python
import jax
import jax.numpy as jnp
from jax import lax
from jax.sharding import Mesh
from jax.sharding import PartitionSpec as P

N_Y, N_Z = 4, 2


def similar(left, right):
    return lax.dot_general(
        left,
        right,
        (((1,), (1,)), ((), ())),
        precision=lax.Precision.HIGH,
        preferred_element_type=jnp.float32,
    )


def lookup(source, indices, first_row):
    position = indices - first_row
    inside = (position >= 0) & (position < source.shape[0])
    picked = jnp.take(source, jnp.clip(position, 0, source.shape[0] - 1), axis=0)
    return jnp.where(inside[:, None], picked, 0.0)


def col_of(y, z):
    return (y % N_Y) * N_Z + z


def y_shift(value, step):
    pairs = [(col_of(y, z), col_of(y + step, z)) for y in range(N_Y) for z in range(N_Z)]
    return lax.ppermute(value, "col", pairs)


def pair_split(value, low):
    halves = value.reshape(2, value.shape[0] // 2, *value.shape[1:])
    return jnp.where(low, halves[0], halves[1]), jnp.where(low, halves[1], halves[0])


def pair_join(mine, other, low):
    return jnp.where(low, jnp.concatenate([mine, other]), jnp.concatenate([other, mine]))


def z_group_shift(value, k):
    if k == 1:
        return lax.ppermute(value, "col", [(c, c ^ 1) for c in range(N_Y * N_Z)])
    if k == 2:
        return lax.ppermute(value, "zl", [(0, 1), (1, 0)])
    n = 2 * N_Y * N_Z
    return lax.ppermute(value, ("zl", "col"), [(i, i ^ (N_Y * N_Z) ^ 1) for i in range(n)])


def group_masked_sum(value):
    here = lax.axis_index("col")
    y, z = here // N_Z, here % N_Z
    g = lax.axis_index("zl") * 2 + z
    quarter = value.shape[0] // N_Y

    def part(k):
        return lax.dynamic_slice_in_dim(value, ((y + k) % N_Y) * quarter, quarter)

    own = part(0)
    for k in range(1, N_Y):
        own = own + y_shift(part(k), k)
    piece = quarter // 4

    def z_part(k):
        return lax.dynamic_slice_in_dim(own, (g ^ k) * piece, piece)

    mine = z_part(0)
    for k in range(1, 4):
        mine = mine + z_group_shift(z_part(k), k)
    received = jnp.stack([mine] + [z_group_shift(mine, k) for k in range(1, 4)])
    own = jnp.take(received, jnp.arange(4) ^ g, axis=0).reshape(own.shape)
    pieces = [own] + [y_shift(own, -k) for k in range(1, N_Y)]
    return jnp.roll(jnp.stack(pieces), y, axis=0).reshape(value.shape)


def all_max_two_rounds(value, axis, n):
    for bits in ((1, 2, 3), (4,)):
        received = [lax.ppermute(value, axis, [(i, i ^ k) for i in range(n)]) for k in bits]
        for other in received:
            value = jnp.maximum(value, other)
    return value


def group_sum_in_order(value):
    here = lax.axis_index("col")
    y, z = here // N_Z, here % N_Z
    g = lax.axis_index("zl") * 2 + z
    received = jnp.stack([value] + [z_group_shift(value, k) for k in range(1, 4)])
    z_sum = jnp.sum(jnp.take(received, jnp.arange(4) ^ g, axis=0), axis=0)
    col_pairs = [[(c, c ^ (2 * k)) for c in range(N_Y * N_Z)] for k in range(1, N_Y)]
    received = jnp.stack([z_sum] + [lax.ppermute(z_sum, "col", pairs) for pairs in col_pairs])
    return jnp.sum(jnp.take(received, jnp.arange(N_Y) ^ y, axis=0), axis=0)


def all_max(value, axis, n):
    bit = 1
    while bit < n:
        value = jnp.maximum(value, lax.ppermute(value, axis, [(i, i ^ bit) for i in range(n)]))
        bit *= 2
    return value


def gather_in_order(parts, axis, n):
    here = lax.axis_index(axis)
    bit = 1
    while bit < n:
        other = lax.ppermute(parts, axis, [(i, i ^ bit) for i in range(n)])
        low = (here & bit) == 0
        parts = jnp.where(low, jnp.concatenate([parts, other]), jnp.concatenate([other, parts]))
        bit *= 2
    return parts


def body(slab_embed, coverage_old, sel_index, cand_index):
    n_xc = 8
    col_id = lax.axis_index("col")
    zl = lax.axis_index("zl")
    half = lax.all_gather(slab_embed, "xc", axis=0, tiled=True)
    first_row = (col_id * 2 + zl) * half.shape[0]
    zl_swap = [(0, 1), (1, 0)]
    both_sel = pair_join(sel_index, lax.ppermute(sel_index, "zl", zl_swap), zl == 0)
    both_cand = pair_join(cand_index, lax.ppermute(cand_index, "zl", zl_swap), zl == 0)
    selected = group_masked_sum(lookup(half, both_sel, first_row))
    chosen = group_masked_sum(lookup(half, both_cand, first_row))
    n_sel = both_sel.shape[0]
    sel_scores = lax.optimization_barrier(similar(selected, half))
    reached = all_max_two_rounds(jnp.max(sel_scores, axis=0), "xc", n_xc)
    old = lax.dynamic_slice_in_dim(coverage_old, zl * half.shape[0], half.shape[0])
    coverage = jnp.maximum(old, reached)
    gain_part = jnp.sum(jnp.maximum(similar(chosen, half) - coverage[None, :], 0.0), axis=1)
    total = group_sum_in_order(gain_part)
    total_gain = lax.dynamic_slice_in_dim(total, zl * cand_index.shape[0], cand_index.shape[0])
    full_coverage = pair_join(coverage, lax.ppermute(coverage, "zl", zl_swap), zl == 0)
    return (full_coverage, total_gain)


def solution(mesh):
    shape = dict(zip(mesh.axis_names, mesh.devices.shape))
    names, sizes = [], []
    for name in mesh.axis_names:
        if name == "row":
            names += ["zl", "xc"]
            sizes += [2, shape["row"] // 2]
        else:
            names.append(name)
            sizes.append(shape[name])
    split = Mesh(mesh.devices.reshape(sizes), tuple(names))
    in_specs = (P(("col", "zl", "xc"), None), P("col"), P(("zl", "xc")), P(("zl", "xc")))
    out_specs = (P("col"), P(("zl", "xc")))
    return jax.shard_map(body, mesh=split, in_specs=in_specs, out_specs=out_specs, check_vma=False)
```

```python
import jax
import jax.numpy as jnp
from jax import lax
from jax.sharding import Mesh
from jax.sharding import PartitionSpec as P

N_Y, N_Z = 4, 2


def similar(left, right):
    return lax.dot_general(
        left,
        right,
        (((1,), (1,)), ((), ())),
        precision=lax.Precision.HIGH,
        preferred_element_type=jnp.float32,
    )


def lookup(source, indices, first_row):
    position = indices - first_row
    inside = (position >= 0) & (position < source.shape[0])
    picked = jnp.take(source, jnp.clip(position, 0, source.shape[0] - 1), axis=0)
    return jnp.where(inside[:, None], picked, 0.0)


def col_of(y, z):
    return (y % N_Y) * N_Z + z


def y_shift(value, step):
    pairs = [(col_of(y, z), col_of(y + step, z)) for y in range(N_Y) for z in range(N_Z)]
    return lax.ppermute(value, "col", pairs)


def pair_split(value, low):
    halves = value.reshape(2, value.shape[0] // 2, *value.shape[1:])
    return jnp.where(low, halves[0], halves[1]), jnp.where(low, halves[1], halves[0])


def pair_join(mine, other, low):
    return jnp.where(low, jnp.concatenate([mine, other]), jnp.concatenate([other, mine]))


def z_group_shift(value, k):
    if k == 1:
        return lax.ppermute(value, "col", [(c, c ^ 1) for c in range(N_Y * N_Z)])
    if k == 2:
        return lax.ppermute(value, "zl", [(0, 1), (1, 0)])
    n = 2 * N_Y * N_Z
    return lax.ppermute(value, ("zl", "col"), [(i, i ^ (N_Y * N_Z) ^ 1) for i in range(n)])


def group_masked_sum(value):
    here = lax.axis_index("col")
    y, z = here // N_Z, here % N_Z
    g = lax.axis_index("zl") * 2 + z
    quarter = value.shape[0] // N_Y

    def part(k):
        return lax.dynamic_slice_in_dim(value, ((y + k) % N_Y) * quarter, quarter)

    own = part(0)
    for k in range(1, N_Y):
        own = own + y_shift(part(k), k)
    piece = quarter // 4

    def z_part(k):
        return lax.dynamic_slice_in_dim(own, (g ^ k) * piece, piece)

    mine = z_part(0)
    for k in range(1, 4):
        mine = mine + z_group_shift(z_part(k), k)
    received = jnp.stack([mine] + [z_group_shift(mine, k) for k in range(1, 4)])
    own = jnp.take(received, jnp.arange(4) ^ g, axis=0).reshape(own.shape)
    pieces = [own] + [y_shift(own, -k) for k in range(1, N_Y)]
    return jnp.roll(jnp.stack(pieces), y, axis=0).reshape(value.shape)


def all_max_two_rounds(value, axis, n):
    for bits in (tuple(range(1, n)),):
        received = [lax.ppermute(value, axis, [(i, i ^ k) for i in range(n)]) for k in bits]
        for other in received:
            value = jnp.maximum(value, other)
    return value


def group_gather_in_order(value):
    here = lax.axis_index("col")
    y, z = here // N_Z, here % N_Z
    g = lax.axis_index("zl") * 2 + z
    received = jnp.stack([value] + [z_group_shift(value, k) for k in range(1, 4)])
    z_ordered = jnp.take(received, jnp.arange(4) ^ g, axis=0)
    col_pairs = [[(c, c ^ (2 * k)) for c in range(N_Y * N_Z)] for k in range(1, N_Y)]
    received = jnp.stack([z_ordered] + [lax.ppermute(z_ordered, "col", pairs) for pairs in col_pairs])
    return jnp.take(received, jnp.arange(N_Y) ^ y, axis=0)


def all_max(value, axis, n):
    bit = 1
    while bit < n:
        value = jnp.maximum(value, lax.ppermute(value, axis, [(i, i ^ bit) for i in range(n)]))
        bit *= 2
    return value


def gather_in_order(parts, axis, n):
    here = lax.axis_index(axis)
    bit = 1
    while bit < n:
        other = lax.ppermute(parts, axis, [(i, i ^ bit) for i in range(n)])
        low = (here & bit) == 0
        parts = jnp.where(low, jnp.concatenate([parts, other]), jnp.concatenate([other, parts]))
        bit *= 2
    return parts


def body(slab_embed, coverage_old, sel_index, cand_index):
    n_xc = 8
    col_id = lax.axis_index("col")
    zl = lax.axis_index("zl")
    half = lax.all_gather(slab_embed, "xc", axis=0, tiled=True)
    first_row = (col_id * 2 + zl) * half.shape[0]
    zl_swap = [(0, 1), (1, 0)]
    both_sel = pair_join(sel_index, lax.ppermute(sel_index, "zl", zl_swap), zl == 0)
    both_cand = pair_join(cand_index, lax.ppermute(cand_index, "zl", zl_swap), zl == 0)
    selected = group_masked_sum(lookup(half, both_sel, first_row))
    chosen = group_masked_sum(lookup(half, both_cand, first_row))
    n_sel = both_sel.shape[0]
    sel_scores = lax.optimization_barrier(similar(selected, half))
    reached = all_max_two_rounds(jnp.max(sel_scores, axis=0), "xc", n_xc)
    old = lax.dynamic_slice_in_dim(coverage_old, zl * half.shape[0], half.shape[0])
    coverage = jnp.maximum(old, reached)
    gain_part = jnp.sum(jnp.maximum(similar(chosen, half) - coverage[None, :], 0.0), axis=1)
    parts = group_gather_in_order(gain_part)
    total = jnp.sum(parts.reshape(-1, gain_part.shape[0]), axis=0)
    total_gain = lax.dynamic_slice_in_dim(total, zl * cand_index.shape[0], cand_index.shape[0])
    full_coverage = pair_join(coverage, lax.ppermute(coverage, "zl", zl_swap), zl == 0)
    return (full_coverage, total_gain)


def solution(mesh):
    shape = dict(zip(mesh.axis_names, mesh.devices.shape))
    names, sizes = [], []
    for name in mesh.axis_names:
        if name == "row":
            names += ["zl", "xc"]
            sizes += [2, shape["row"] // 2]
        else:
            names.append(name)
            sizes.append(shape[name])
    split = Mesh(mesh.devices.reshape(sizes), tuple(names))
    in_specs = (P(("col", "zl", "xc"), None), P("col"), P(("zl", "xc")), P(("zl", "xc")))
    out_specs = (P("col"), P(("zl", "xc")))
    return jax.shard_map(body, mesh=split, in_specs=in_specs, out_specs=out_specs, check_vma=False)
```
